256 devices in a mesh: lat: 8 (over z), lev: 32 (over x, y, core).
Axes of the slice: x: 4, y: 4, z: 8, core: 2. Of those that a mesh axis runs over, the one named last changes fastest.
Arguments:
- spec_in: bfloat16 [32, 640, 1281], P('lev', 'lat'), may hold values from -6 to 6
- legendre: bfloat16 [640, 1280, 1281], P('lat', 'lev'), may hold values from -0.15625 to 0.15625
- gauss_weights: float32 [1280], P('lev'), may hold values from 0.1 to 1
- row_points: int32 [2, 1280], P(None, 'lev'), may hold values from 4 to 5120
Outputs:
- spec_out: bfloat16 [32, 640, 1281], P('lev', 'lat')
The draws below stay inside these ranges and needn't reach their ends.
All inputs are finite; a program needn't handle non-finite values.
Results may differ from the reference program's by a relative error of at most 0.02.
Values may be sent and summed in bfloat16 or wider, within the bound.
No kernel may reach another device: no remote copies, remote signals or barrier semaphores. Data moves between devices by JAX's collectives and lax.ppermute only.
A program may use at most 128 MiB of HBM per device.

```python
import math
import jax
import jax.numpy as jnp
from jax import lax

NLON = 5120
PAIRS = 640
PACKED = 1281
HALF = 1280
CHANNELS = 32
N_LEV = 32


def with_ends(values, key, low, top_value):
    dims = values.shape
    spot = [jax.random.randint(jax.random.fold_in(key, axis), (), 0, dims[axis]) for axis in range(len(dims))]
    values = values.at[tuple(spot)].set(low)
    longest = dims.index(max(dims))
    spot[longest] = (spot[longest] + 1) % dims[longest]
    return values.at[tuple(spot)].set(top_value)


def block_scale(key, shape, shards, least, high):
    def one(axis_at, parts):
        heights = jax.random.uniform(jax.random.fold_in(jax.random.fold_in(key, 6), axis_at), (parts,), jnp.float32, least / len(shards), high / len(shards))
        return jnp.repeat(jnp.exp(heights), shape[axis_at] // parts).reshape((-1,) + (1,) * (len(shape) - axis_at - 1))

    gain = one(*shards[0])
    for cut in shards[1:]:
        gain = gain * one(*cut)
    return gain


def noise(stream_key, shape, scale, bound, shards=(), kind=jnp.bfloat16):
    values = jax.random.normal(stream_key, shape, jnp.float32) * scale
    if len(shards) > 0:
        values = block_scale(stream_key, shape, shards, -0.22, 0.18) * values
    return jnp.clip(values, min=-bound, max=bound).astype(kind)


def setup_inputs(seed: int = 0) -> dict:
    seeds = jax.random.split(jax.random.key(seed), 5)
    return {
        "spec_in": noise(seeds[0], (CHANNELS, PAIRS, PACKED), 1.0, 6.0, ((0, 32), (1, 8))),
        "legendre": noise(seeds[1], (PAIRS, HALF, PACKED), PACKED ** -0.5, 0.15625, ((0, 8), (1, 32))),
        "gauss_weights": jnp.clip(jnp.exp(math.log(1.0) - 2.3025851 * jax.random.uniform(seeds[2], (HALF,), jnp.float32) ** block_scale(seeds[2], (HALF,), ((0, 32),), -0.2, 0.2)), 0.1, 1.0),
        "row_points": with_ends(jax.random.randint(seeds[3], (2, HALF), 4, NLON + 1), jax.random.fold_in(seeds[3], 1), 4, NLON).astype(jnp.int32),
    }


SLOT_CODES = (0, 0, 1, 1)
PARITY_CODES = (0, 1, 0, 1)

def pair_masks(first_pair, pair_count, packed):
    pair_ids = first_pair + jnp.arange(pair_count, dtype=jnp.int32)
    positions = jnp.arange(packed, dtype=jnp.int32)
    boundary = packed - 1 - pair_ids
    in_second = (positions[None, :] >= boundary[:, None]).astype(jnp.int32)
    degree = positions[None, :] - in_second * boundary[:, None]
    parity = degree % 2
    slot_codes = jnp.array(SLOT_CODES, dtype=jnp.int32)
    parity_codes = jnp.array(PARITY_CODES, dtype=jnp.int32)
    return (in_second[:, :, None] == slot_codes) & (parity[:, :, None] == parity_codes)

def wave_tables(total_pairs, truncation):
    pair_ids = jnp.arange(total_pairs, dtype=jnp.int32)
    wavenumbers = jnp.stack([pair_ids, truncation - pair_ids], axis=1)
    longitudes = jnp.arange(NLON, dtype=jnp.int32)
    phases = wavenumbers[:, :, None] * longitudes[None, None, :] % NLON
    angles = phases.astype(jnp.float32) * (2.0 * math.pi / NLON)
    return (jnp.cos(angles).astype(jnp.bfloat16), jnp.sin(angles).astype(jnp.bfloat16), wavenumbers)

def fourier_work(spectrum, row_counts, cosines, sines, wavenumbers, truncation):
    kept_mask = (2 * wavenumbers[:, None, :] < row_counts[None, :, None]).astype(jnp.float32)
    masked = spectrum.astype(jnp.float32) * kept_mask[..., None]
    half_channels = spectrum.shape[-1] // 2
    levels = half_channels // 2
    real_part = masked[..., :half_channels]
    imag_part = masked[..., half_channels:]
    grid_values = jnp.einsum('plsf,psk->lfk', real_part, cosines)
    grid_values = (grid_values - jnp.einsum('plsf,psk->lfk', imag_part, sines)) * (1.0 / math.sqrt(truncation + 1))
    vortex = grid_values[:, :levels]
    divergence = grid_values[:, levels:]
    products = jnp.concatenate([vortex * divergence, 0.5 * (vortex * vortex - divergence * divergence)], axis=1)
    products = lax.optimization_barrier(products.astype(jnp.bfloat16)).astype(jnp.float32)
    scale_back = 4.0 / math.sqrt(NLON)
    real_out = jnp.einsum('lfk,psk->plsf', products, cosines) * scale_back
    imag_out = -jnp.einsum('lfk,psk->plsf', products, sines) * scale_back
    return (jnp.concatenate([real_out, imag_out], axis=-1) * kept_mask[..., None]).astype(jnp.bfloat16)

def reference(spec_in, legendre, gauss_weights, row_points):
    channels, pair_total, packed = spec_in.shape
    half_lats = legendre.shape[1]
    truncation = packed - 2
    tile_size = 8
    tile_count = pair_total // tile_size
    selector = pair_masks(0, pair_total, packed).astype(jnp.float32)
    select_tiles = selector.reshape(tile_count, tile_size, packed, 4)
    legendre_tiles = legendre.reshape(tile_count, tile_size, half_lats, packed)
    spectral_tiles = jnp.moveaxis(spec_in.reshape(channels, tile_count, tile_size, packed), 1, 0)

    def inverse_tile(inputs):
        legendre_tile, spectral_tile, select_tile = inputs
        spread = spectral_tile.astype(jnp.float32)[None] * jnp.moveaxis(select_tile, 2, 0)[:, None]
        legendre_sums = jnp.einsum('pjq,xcpq->pjxc', legendre_tile.astype(jnp.float32), spread)
        even_part = legendre_sums[:, :, 0::2]
        odd_part = legendre_sums[:, :, 1::2]
        return jnp.concatenate([even_part + odd_part, even_part - odd_part], axis=1).astype(jnp.bfloat16)
    fourier = lax.map(inverse_tile, (legendre_tiles, spectral_tiles, select_tiles))
    fourier = fourier.reshape(pair_total, 2 * half_lats, 2, channels)
    cosines, sines, wavenumbers = wave_tables(pair_total, truncation)
    cos_wide = cosines.astype(jnp.float32)
    sin_wide = sines.astype(jnp.float32)
    lat_block = 16
    block_count = 2 * half_lats // lat_block
    fourier_blocks = jnp.moveaxis(fourier.reshape(pair_total, block_count, lat_block, 2, channels), 1, 0)
    row_blocks = row_points.reshape(block_count, lat_block)

    def grid_block(inputs):
        spectrum, row_counts = inputs
        return fourier_work(spectrum, row_counts, cos_wide, sin_wide, wavenumbers, truncation)
    returned = lax.map(grid_block, (fourier_blocks, row_blocks))
    back = jnp.moveaxis(returned, 0, 1).reshape(pair_total, 2 * half_lats, 2, channels)
    north_rows = back[:, :half_lats].astype(jnp.float32)
    south_rows = back[:, half_lats:].astype(jnp.float32)
    weights = gauss_weights[None, :, None, None]
    weighted = jnp.stack([weights * (north_rows + south_rows), weights * (north_rows - south_rows)], axis=3)
    weighted = weighted.reshape(pair_total, half_lats, 4, channels)
    weighted = lax.optimization_barrier(weighted.astype(jnp.bfloat16))
    slab = half_lats // N_LEV
    legendre_groups = legendre.reshape(tile_count, tile_size, N_LEV, slab, packed)
    weighted_groups = weighted.reshape(tile_count, tile_size, N_LEV, slab, 4, channels)

    def direct_tile(inputs):
        legendre_tile, weighted_tile, select_tile = inputs

        def add_group(running, group_inputs):
            legendre_group, weighted_group = group_inputs
            full_sums = jnp.einsum('pjq,pjxc->pqxc', legendre_group.astype(jnp.float32), weighted_group.astype(jnp.float32))
            picked = jnp.moveaxis(lax.optimization_barrier(jnp.sum(full_sums * select_tile[:, :, :, None], axis=2)), 2, 0)
            rounded = lax.optimization_barrier(picked.astype(jnp.bfloat16))
            return (running + rounded.astype(jnp.float32), None)
        start_sum = jnp.zeros((channels, tile_size, packed), jnp.float32)
        total_sum = lax.scan(add_group, start_sum, (jnp.moveaxis(legendre_tile, 1, 0), jnp.moveaxis(weighted_tile, 1, 0)))[0]
        return total_sum
    summed = lax.map(direct_tile, (legendre_groups, weighted_groups, select_tiles))
    return jnp.moveaxis(summed, 0, 1).reshape(channels, pair_total, packed).astype(jnp.bfloat16)
```

```python
import math

import jax
import jax.numpy as jnp
from jax import lax
from jax.sharding import PartitionSpec as P

NLON = 5120


SLOT_CODES = (0, 0, 1, 1)
PARITY_CODES = (0, 1, 0, 1)


def pair_masks(first_pair, pair_count, packed):
    pair_ids = first_pair + jnp.arange(pair_count, dtype=jnp.int32)
    positions = jnp.arange(packed, dtype=jnp.int32)
    boundary = packed - 1 - pair_ids
    in_second = (positions[None, :] >= boundary[:, None]).astype(jnp.int32)
    degree = positions[None, :] - in_second * boundary[:, None]
    parity = degree % 2
    slot_codes = jnp.array(SLOT_CODES, dtype=jnp.int32)
    parity_codes = jnp.array(PARITY_CODES, dtype=jnp.int32)
    return (in_second[:, :, None] == slot_codes) & (parity[:, :, None] == parity_codes)


def wave_tables(total_pairs, truncation):
    pair_ids = jnp.arange(total_pairs, dtype=jnp.int32)
    wavenumbers = jnp.stack([pair_ids, truncation - pair_ids], axis=1)
    flat = wavenumbers.reshape(-1)
    inner = 64
    outer = NLON // inner
    step = 2.0 * math.pi / NLON
    coarse = (flat[:, None] * (inner * jnp.arange(outer, dtype=jnp.int32))[None, :]) % NLON
    fine = (flat[:, None] * jnp.arange(inner, dtype=jnp.int32)[None, :]) % NLON
    coarse_angle = coarse.astype(jnp.float32) * step
    fine_angle = fine.astype(jnp.float32) * step
    cos_a = jnp.cos(coarse_angle)[:, :, None]
    sin_a = jnp.sin(coarse_angle)[:, :, None]
    cos_b = jnp.cos(fine_angle)[:, None, :]
    sin_b = jnp.sin(fine_angle)[:, None, :]
    rows = flat.shape[0]
    cosines = (cos_a * cos_b - sin_a * sin_b).reshape(rows, NLON).astype(jnp.bfloat16)
    sines = (sin_a * cos_b + cos_a * sin_b).reshape(rows, NLON).astype(jnp.bfloat16)
    table = lax.optimization_barrier(jnp.concatenate([cosines, sines], axis=0))
    return table, wavenumbers


def fourier_work(spectrum, row_counts, table, wavenumbers, truncation):
    pairs, lats, slots, channels = spectrum.shape
    kept_mask = (2 * wavenumbers[:, None, :] < row_counts[None, :, None]).astype(jnp.bfloat16)
    masked = spectrum * kept_mask[..., None]
    half_channels = channels // 2
    levels = half_channels // 2
    rows = lats * half_channels
    waves = pairs * slots
    flat = jnp.transpose(masked, (1, 3, 0, 2)).reshape(lats, channels, waves)
    real_part = flat[:, :half_channels].reshape(rows, waves)
    imag_part = flat[:, half_channels:].reshape(rows, waves)
    lhs = jnp.concatenate([real_part, -imag_part], axis=1)
    grid_values = jnp.dot(lhs, table, preferred_element_type=jnp.float32) * (
        1.0 / math.sqrt(truncation + 1)
    )
    grid_values = grid_values.reshape(lats, half_channels, NLON)
    vortex = grid_values[:, :levels]
    divergence = grid_values[:, levels:]
    products = jnp.concatenate(
        [vortex * divergence, 0.5 * (vortex * vortex - divergence * divergence)], axis=1
    ).astype(jnp.bfloat16)
    scale_back = 4.0 / math.sqrt(NLON)
    back = lax.dot_general(
        products.reshape(rows, NLON),
        table,
        (((1,), (1,)), ((), ())),
        preferred_element_type=jnp.float32,
    )
    real_out = back[:, :waves] * scale_back
    imag_out = back[:, waves:] * (-scale_back)
    out = jnp.concatenate(
        [real_out.reshape(lats, half_channels, waves), imag_out.reshape(lats, half_channels, waves)],
        axis=1,
    )
    out = jnp.transpose(out.reshape(lats, channels, pairs, slots), (2, 0, 3, 1))
    return (out * kept_mask[..., None].astype(jnp.float32)).astype(jnp.bfloat16)


def local(spec_in, legendre, gauss_weights, row_points):
    pair_count, lat_count, packed = legendre.shape
    truncation = packed - 2
    groups = lax.axis_size("lat")
    local_channels = spec_in.shape[0]
    channels = local_channels * lax.axis_size("lev")
    tile_size = math.gcd(pair_count, 8)
    tile_count = pair_count // tile_size
    first_pair = lax.axis_index("lat") * pair_count
    selector = pair_masks(first_pair, pair_count, packed)
    select_half = selector.astype(jnp.bfloat16).reshape(tile_count, tile_size, packed, 4)
    select_full = selector.astype(jnp.float32).reshape(tile_count, tile_size, packed, 4)
    legendre_tiles = legendre.reshape(tile_count, tile_size, lat_count, packed)
    gathered = lax.all_gather(spec_in, "lev", axis=0, tiled=True)
    piece_width = gathered.shape[0]
    spectral = jnp.moveaxis(gathered.reshape(piece_width, tile_count, tile_size, packed), 1, 0)

    def inverse_tile(inputs):
        legendre_tile, spectral_tile, select_tile = inputs
        spread = spectral_tile[None] * jnp.moveaxis(select_tile, 2, 0)[:, None]
        return jnp.einsum(
            "pjq,xcpq->pjxc", legendre_tile, spread, preferred_element_type=jnp.float32
        )

    tile_sums = lax.map(inverse_tile, (legendre_tiles, spectral, select_half))
    legendre_sums = tile_sums.reshape(pair_count, lat_count, 4, piece_width)
    even_part = legendre_sums[:, :, 0::2]
    odd_part = legendre_sums[:, :, 1::2]
    fourier = jnp.concatenate([even_part + odd_part, even_part - odd_part], axis=1).astype(
        jnp.bfloat16
    )
    table, wavenumbers = wave_tables(pair_count * groups, truncation)
    local_rows = row_points.reshape(1, 2 * lat_count)
    band_lats = 2 * lat_count // groups
    lat_rows = lax.all_to_all(fourier, "lat", split_axis=1, concat_axis=0, tiled=True)
    my_rows = lax.dynamic_slice_in_dim(local_rows[0], lax.axis_index("lat") * band_lats, band_lats)
    answered = fourier_work(lat_rows, my_rows, table, wavenumbers, truncation)
    answered = answered.reshape(groups, pair_count, band_lats, 2, channels)
    returned = lax.all_to_all(answered, "lat", split_axis=0, concat_axis=0, tiled=True)
    back = jnp.moveaxis(returned, 0, 1).reshape(pair_count, 2 * lat_count, 2, channels)
    north_rows = back[:, :lat_count].astype(jnp.float32)
    south_rows = back[:, lat_count:].astype(jnp.float32)
    weights = gauss_weights[None, :, None, None]
    weighted = jnp.stack(
        [weights * (north_rows + south_rows), weights * (north_rows - south_rows)], axis=3
    )
    weighted = weighted.reshape(pair_count, lat_count, 4, channels).astype(jnp.bfloat16)
    part_tiles = weighted.reshape(
        tile_count, tile_size, lat_count, 4, local_channels * lax.axis_size("lev")
    )

    def direct_tile(inputs):
        legendre_tile, weighted_tile, select_tile = inputs
        full_sums = jnp.einsum(
            "pjq,pjxc->pqxc", legendre_tile, weighted_tile, preferred_element_type=jnp.float32
        )
        picked = jnp.sum(full_sums * select_tile[:, :, :, None], axis=2)
        return jnp.moveaxis(picked, 2, 0)

    picked_tiles = lax.map(direct_tile, (legendre_tiles, part_tiles, select_full))
    return lax.psum_scatter(
        jnp.moveaxis(picked_tiles, 0, 1)
        .reshape(local_channels * lax.axis_size("lev"), pair_count, packed)
        .astype(jnp.bfloat16),
        "lev",
        scatter_dimension=0,
        tiled=True,
    )


def solution(mesh):
    return jax.shard_map(
        local,
        mesh=mesh,
        in_specs=(P("lev", "lat", None), P("lat", "lev", None), P("lev"), P(None, "lev")),
        out_specs=P("lev", "lat", None),
        check_vma=False,
    )
```

```python
import math

import jax
import jax.numpy as jnp
from jax import lax
from jax.experimental import pallas as pl
from jax.sharding import PartitionSpec as P

NLON = 5120


def wave_tables(total_pairs, truncation):
    pair_ids = jnp.arange(total_pairs, dtype=jnp.int32)
    wavenumbers = jnp.stack([pair_ids, truncation - pair_ids], axis=1)
    flat = wavenumbers.reshape(-1)
    inner = 64
    outer = NLON // inner
    step = 2.0 * math.pi / NLON
    coarse = (flat[:, None] * (inner * jnp.arange(outer, dtype=jnp.int32))[None, :]) % NLON
    fine = (flat[:, None] * jnp.arange(inner, dtype=jnp.int32)[None, :]) % NLON
    coarse_angle = coarse.astype(jnp.float32) * step
    fine_angle = fine.astype(jnp.float32) * step
    cos_a = jnp.cos(coarse_angle)[:, :, None]
    sin_a = jnp.sin(coarse_angle)[:, :, None]
    cos_b = jnp.cos(fine_angle)[:, None, :]
    sin_b = jnp.sin(fine_angle)[:, None, :]
    rows = flat.shape[0]
    cosines = (cos_a * cos_b - sin_a * sin_b).reshape(rows, NLON).astype(jnp.bfloat16)
    sines = (sin_a * cos_b + cos_a * sin_b).reshape(rows, NLON).astype(jnp.bfloat16)
    table = lax.optimization_barrier(jnp.concatenate([cosines, sines], axis=0))
    return table, wavenumbers


def fourier_work(spectrum, row_counts, table, wavenumbers, truncation):
    pairs, lats, slots, channels = spectrum.shape
    kept_mask = (2 * wavenumbers[:, None, :] < row_counts[None, :, None]).astype(jnp.bfloat16)
    masked = spectrum * kept_mask[..., None]
    half_channels = channels // 2
    levels = half_channels // 2
    rows = lats * half_channels
    waves = pairs * slots
    flat = jnp.transpose(masked, (1, 3, 0, 2)).reshape(lats, channels, waves)
    real_part = flat[:, :half_channels].reshape(rows, waves)
    imag_part = flat[:, half_channels:].reshape(rows, waves)
    lhs = jnp.concatenate([real_part, -imag_part], axis=1)
    grid_values = jnp.dot(lhs, table, preferred_element_type=jnp.float32) * (
        1.0 / math.sqrt(truncation + 1)
    )
    grid_values = grid_values.reshape(lats, half_channels, NLON)
    vortex = grid_values[:, :levels]
    divergence = grid_values[:, levels:]
    products = jnp.concatenate(
        [vortex * divergence, 0.5 * (vortex * vortex - divergence * divergence)], axis=1
    ).astype(jnp.bfloat16)
    scale_back = 4.0 / math.sqrt(NLON)
    back = lax.dot_general(
        products.reshape(rows, NLON),
        table,
        (((1,), (1,)), ((), ())),
        preferred_element_type=jnp.float32,
    )
    real_out = back[:, :waves] * scale_back
    imag_out = back[:, waves:] * (-scale_back)
    out = jnp.concatenate(
        [real_out.reshape(lats, half_channels, waves), imag_out.reshape(lats, half_channels, waves)],
        axis=1,
    )
    out = jnp.transpose(out.reshape(lats, channels, pairs, slots), (2, 0, 3, 1))
    return (out * kept_mask[..., None].astype(jnp.float32)).astype(jnp.bfloat16)


def slot_codes(first_pair, pair_count, packed):
    pair_ids = first_pair + jnp.arange(pair_count, dtype=jnp.int32)
    positions = jnp.arange(packed, dtype=jnp.int32)
    boundary = packed - 1 - pair_ids
    in_second = (positions[None, :] >= boundary[:, None]).astype(jnp.int32)
    degree = positions[None, :] - in_second * boundary[:, None]
    return (2 * in_second + degree % 2).reshape(pair_count, 1, packed)


def inverse_kernel(leg_ref, spec_ref, code_ref, out_ref):
    block = leg_ref.shape[0]

    def one_pair(pp, carry):
        legendre_pair = leg_ref[pp]
        spectrum = spec_ref[pp]
        code = code_ref[pp]
        slot = code // 2
        sign = (1 - 2 * (code % 2)).astype(spectrum.dtype)
        zero = jnp.zeros_like(spectrum)
        first = jnp.where(slot == 0, spectrum, zero)
        second = jnp.where(slot == 1, spectrum, zero)
        masked = jnp.concatenate([first, second, first * sign, second * sign], axis=0)
        sums = lax.dot_general(
            legendre_pair, masked, (((1,), (1,)), ((), ())), preferred_element_type=jnp.float32
        )
        half = sums.shape[1] // 2
        out_ref[pp] = jnp.concatenate([sums[:, :half], sums[:, half:]], axis=0).astype(
            out_ref.dtype
        )
        return carry

    lax.fori_loop(0, block, one_pair, 0)


def direct_kernel(leg_ref, weight_ref, code_ref, out_ref):
    block = leg_ref.shape[0]
    channels = out_ref.shape[1]

    def one_pair(pp, carry):
        full = jnp.dot(weight_ref[pp], leg_ref[pp], preferred_element_type=jnp.float32)
        code = code_ref[pp]
        picked = jnp.where(code == 0, full[:channels], 0.0)
        for x in range(1, 4):
            picked = picked + jnp.where(code == x, full[x * channels : (x + 1) * channels], 0.0)
        out_ref[pp] = picked.astype(out_ref.dtype)
        return carry

    lax.fori_loop(0, block, one_pair, 0)


def legendre_inverse(legendre, spectrum, codes, block):
    pair_count, lat_count, packed = legendre.shape
    channels = spectrum.shape[1]
    return pl.pallas_call(
        inverse_kernel,
        grid=(pair_count // block,),
        in_specs=[
            pl.BlockSpec((block, lat_count, packed), lambda i: (i, 0, 0)),
            pl.BlockSpec((block, channels, packed), lambda i: (i, 0, 0)),
            pl.BlockSpec((block, 1, packed), lambda i: (i, 0, 0)),
        ],
        out_specs=pl.BlockSpec((block, 2 * lat_count, 2 * channels), lambda i: (i, 0, 0)),
        out_shape=jax.ShapeDtypeStruct((pair_count, 2 * lat_count, 2 * channels), jnp.bfloat16),
    )(legendre, spectrum, codes)


def legendre_direct(legendre, weights, codes, block):
    pair_count, lat_count, packed = legendre.shape
    rows = weights.shape[1]
    channels = rows // 4
    return pl.pallas_call(
        direct_kernel,
        grid=(pair_count // block,),
        in_specs=[
            pl.BlockSpec((block, lat_count, packed), lambda i: (i, 0, 0)),
            pl.BlockSpec((block, rows, lat_count), lambda i: (i, 0, 0)),
            pl.BlockSpec((block, 1, packed), lambda i: (i, 0, 0)),
        ],
        out_specs=pl.BlockSpec((block, channels, packed), lambda i: (i, 0, 0)),
        out_shape=jax.ShapeDtypeStruct((pair_count, channels, packed), jnp.bfloat16),
    )(legendre, weights, codes)


def local(spec_in, legendre, gauss_weights, row_points):
    pair_count, lat_count, packed = legendre.shape
    truncation = packed - 2
    groups = lax.axis_size("lat")
    local_channels = spec_in.shape[0]
    channels = local_channels * lax.axis_size("lev")
    block = math.gcd(pair_count, 8)
    first_pair = lax.axis_index("lat") * pair_count
    codes = slot_codes(first_pair, pair_count, packed)
    gathered = lax.all_gather(spec_in[0], "lev", axis=1, tiled=False)
    fourier = legendre_inverse(legendre, gathered, codes, block)
    fourier = fourier.reshape(pair_count, 2 * lat_count, 2, channels)
    table, wavenumbers = wave_tables(pair_count * groups, truncation)
    local_rows = row_points.reshape(1, 2 * lat_count)
    band_lats = 2 * lat_count // groups
    lat_rows = lax.all_to_all(fourier, "lat", split_axis=1, concat_axis=0, tiled=True)
    my_rows = lax.dynamic_slice_in_dim(local_rows[0], lax.axis_index("lat") * band_lats, band_lats)
    answered = fourier_work(lat_rows, my_rows, table, wavenumbers, truncation)
    answered = answered.reshape(groups, pair_count, band_lats, 2, channels)
    returned = lax.all_to_all(answered, "lat", split_axis=0, concat_axis=0, tiled=True)
    back = jnp.moveaxis(returned, 0, 1).reshape(pair_count, 2 * lat_count, 2, channels)
    north_rows = back[:, :lat_count].astype(jnp.float32)
    south_rows = back[:, lat_count:].astype(jnp.float32)
    weights = gauss_weights[None, :, None, None]
    weighted = jnp.stack(
        [weights * (north_rows + south_rows), weights * (north_rows - south_rows)], axis=3
    )
    weighted = weighted.reshape(pair_count, lat_count, 4 * channels).astype(jnp.bfloat16)
    weighted = jnp.swapaxes(weighted, 1, 2)
    partial = legendre_direct(legendre, weighted, codes, block)
    summed = lax.psum_scatter(partial, "lev", scatter_dimension=1, tiled=True)
    return jnp.swapaxes(summed, 0, 1)


def solution(mesh):
    return jax.shard_map(
        local,
        mesh=mesh,
        in_specs=(P("lev", "lat", None), P("lat", "lev", None), P("lev"), P(None, "lev")),
        out_specs=P("lev", "lat", None),
        check_vma=False,
    )
```

```python
import math

import jax
import jax.numpy as jnp
from jax import lax
from jax.experimental import pallas as pl
from jax.sharding import PartitionSpec as P

NLON = 5120


def wave_tables(total_pairs, truncation):
    pair_ids = jnp.arange(total_pairs, dtype=jnp.int32)
    wavenumbers = jnp.stack([pair_ids, truncation - pair_ids], axis=1)
    flat = wavenumbers.reshape(-1)
    inner = 64
    outer = NLON // inner
    step = 2.0 * math.pi / NLON
    coarse = (flat[:, None] * (inner * jnp.arange(outer, dtype=jnp.int32))[None, :]) % NLON
    fine = (flat[:, None] * jnp.arange(inner, dtype=jnp.int32)[None, :]) % NLON
    coarse_angle = coarse.astype(jnp.float32) * step
    fine_angle = fine.astype(jnp.float32) * step
    cos_a = jnp.cos(coarse_angle)[:, :, None]
    sin_a = jnp.sin(coarse_angle)[:, :, None]
    cos_b = jnp.cos(fine_angle)[:, None, :]
    sin_b = jnp.sin(fine_angle)[:, None, :]
    rows = flat.shape[0]
    cosines = (cos_a * cos_b - sin_a * sin_b).reshape(rows, NLON).astype(jnp.bfloat16)
    sines = (sin_a * cos_b + cos_a * sin_b).reshape(rows, NLON).astype(jnp.bfloat16)
    table = lax.optimization_barrier(jnp.concatenate([cosines, sines], axis=0))
    return table, wavenumbers


def fourier_work(spectrum, row_counts, table, wavenumbers, truncation):
    pairs, lats, slots, channels = spectrum.shape
    kept_mask = (2 * wavenumbers[:, None, :] < row_counts[None, :, None]).astype(jnp.bfloat16)
    masked = spectrum * kept_mask[..., None]
    half_channels = channels // 2
    levels = half_channels // 2
    rows = lats * half_channels
    waves = pairs * slots
    flat = jnp.transpose(masked, (1, 3, 0, 2)).reshape(lats, channels, waves)
    real_part = flat[:, :half_channels].reshape(rows, waves)
    imag_part = flat[:, half_channels:].reshape(rows, waves)
    lhs = jnp.concatenate([real_part, -imag_part], axis=1)
    grid_values = jnp.dot(lhs, table, preferred_element_type=jnp.float32) * (
        1.0 / math.sqrt(truncation + 1)
    )
    grid_values = grid_values.reshape(lats, half_channels, NLON)
    vortex = grid_values[:, :levels]
    divergence = grid_values[:, levels:]
    products = jnp.concatenate(
        [vortex * divergence, 0.5 * (vortex * vortex - divergence * divergence)], axis=1
    ).astype(jnp.bfloat16)
    scale_back = 4.0 / math.sqrt(NLON)
    back = lax.dot_general(
        products.reshape(rows, NLON),
        table,
        (((1,), (1,)), ((), ())),
        preferred_element_type=jnp.float32,
    )
    real_out = back[:, :waves] * scale_back
    imag_out = back[:, waves:] * (-scale_back)
    out = jnp.concatenate(
        [real_out.reshape(lats, half_channels, waves), imag_out.reshape(lats, half_channels, waves)],
        axis=1,
    )
    out = jnp.transpose(out.reshape(lats, channels, pairs, slots), (2, 0, 3, 1))
    return (out * kept_mask[..., None].astype(jnp.float32)).astype(jnp.bfloat16)


def slot_codes(first_pair, pair_count, packed):
    pair_ids = first_pair + jnp.arange(pair_count, dtype=jnp.int32)
    positions = jnp.arange(packed, dtype=jnp.int32)
    boundary = packed - 1 - pair_ids
    in_second = (positions[None, :] >= boundary[:, None]).astype(jnp.int32)
    degree = positions[None, :] - in_second * boundary[:, None]
    return (2 * in_second + degree % 2).reshape(pair_count, 1, packed)


def inverse_kernel(leg_ref, spec_ref, code_ref, out_ref):
    block = leg_ref.shape[0]

    for pp in range(block):
        legendre_pair = leg_ref[pp]
        spectrum = spec_ref[:, pp, :]
        code = code_ref[pp]
        slot = code // 2
        sign = (1 - 2 * (code % 2)).astype(spectrum.dtype)
        zero = jnp.zeros_like(spectrum)
        first = jnp.where(slot == 0, spectrum, zero)
        second = jnp.where(slot == 1, spectrum, zero)
        masked = jnp.concatenate([first, second, first * sign, second * sign], axis=0)
        sums = lax.dot_general(
            legendre_pair, masked, (((1,), (1,)), ((), ())), preferred_element_type=jnp.float32
        )
        half = sums.shape[1] // 2
        out_ref[pp] = jnp.concatenate([sums[:, :half], sums[:, half:]], axis=0).astype(
            out_ref.dtype
        )


def direct_kernel(leg_ref, weight_ref, code_ref, out_ref):
    block = leg_ref.shape[0]
    channels = out_ref.shape[0]

    for pp in range(block):
        full = jnp.dot(weight_ref[pp], leg_ref[pp], preferred_element_type=jnp.float32)
        code = code_ref[pp]
        picked = jnp.where(code == 0, full[:channels], 0.0)
        for x in range(1, 4):
            picked = picked + jnp.where(code == x, full[x * channels : (x + 1) * channels], 0.0)
        out_ref[:, pp, :] = picked.astype(out_ref.dtype)


def legendre_inverse(legendre, spectrum, codes, block):
    pair_count, lat_count, packed = legendre.shape
    channels = spectrum.shape[0]
    return pl.pallas_call(
        inverse_kernel,
        grid=(pair_count // block,),
        in_specs=[
            pl.BlockSpec((block, lat_count, packed), lambda i: (i, 0, 0)),
            pl.BlockSpec((channels, block, packed), lambda i: (0, i, 0)),
            pl.BlockSpec((block, 1, packed), lambda i: (i, 0, 0)),
        ],
        out_specs=pl.BlockSpec((block, 2 * lat_count, 2 * channels), lambda i: (i, 0, 0)),
        out_shape=jax.ShapeDtypeStruct((pair_count, 2 * lat_count, 2 * channels), jnp.bfloat16),
    )(legendre, spectrum, codes)


def legendre_direct(legendre, weights, codes, block):
    pair_count, lat_count, packed = legendre.shape
    rows = weights.shape[1]
    channels = rows // 4
    return pl.pallas_call(
        direct_kernel,
        grid=(pair_count // block,),
        in_specs=[
            pl.BlockSpec((block, lat_count, packed), lambda i: (i, 0, 0)),
            pl.BlockSpec((block, rows, lat_count), lambda i: (i, 0, 0)),
            pl.BlockSpec((block, 1, packed), lambda i: (i, 0, 0)),
        ],
        out_specs=pl.BlockSpec((channels, block, packed), lambda i: (0, i, 0)),
        out_shape=jax.ShapeDtypeStruct((channels, pair_count, packed), jnp.bfloat16),
    )(legendre, weights, codes)


def local(spec_in, legendre, gauss_weights, row_points):
    pair_count, lat_count, packed = legendre.shape
    truncation = packed - 2
    groups = lax.axis_size("lat")
    local_channels = spec_in.shape[0]
    channels = local_channels * lax.axis_size("lev")
    block = math.gcd(pair_count, 8)
    first_pair = lax.axis_index("lat") * pair_count
    codes = slot_codes(first_pair, pair_count, packed)
    gathered = lax.all_gather(spec_in, "lev", axis=0, tiled=True)
    fourier = legendre_inverse(legendre, gathered, codes, block)
    fourier = fourier.reshape(pair_count, 2 * lat_count, 2, channels)
    table, wavenumbers = wave_tables(pair_count * groups, truncation)
    local_rows = row_points.reshape(1, 2 * lat_count)
    band_lats = 2 * lat_count // groups
    lat_rows = lax.all_to_all(fourier, "lat", split_axis=1, concat_axis=0, tiled=True)
    my_rows = lax.dynamic_slice_in_dim(local_rows[0], lax.axis_index("lat") * band_lats, band_lats)
    answered = fourier_work(lat_rows, my_rows, table, wavenumbers, truncation)
    answered = answered.reshape(groups, pair_count, band_lats, 2, channels)
    returned = lax.all_to_all(answered, "lat", split_axis=0, concat_axis=0, tiled=True)
    back = jnp.moveaxis(returned, 0, 1).reshape(pair_count, 2 * lat_count, 2, channels)
    north_rows = back[:, :lat_count].astype(jnp.float32)
    south_rows = back[:, lat_count:].astype(jnp.float32)
    weights = gauss_weights[None, :, None, None]
    weighted = jnp.stack(
        [weights * (north_rows + south_rows), weights * (north_rows - south_rows)], axis=3
    )
    weighted = weighted.reshape(pair_count, lat_count, 4 * channels).astype(jnp.bfloat16)
    weighted = jnp.swapaxes(weighted, 1, 2)
    partial = legendre_direct(legendre, weighted, codes, block)
    return lax.psum_scatter(partial, "lev", scatter_dimension=0, tiled=True)


def solution(mesh):
    return jax.shard_map(
        local,
        mesh=mesh,
        in_specs=(P("lev", "lat", None), P("lat", "lev", None), P("lev"), P(None, "lev")),
        out_specs=P("lev", "lat", None),
        check_vma=False,
    )
```

```python
import math

import jax
import jax.numpy as jnp
from jax import lax
from jax.experimental import pallas as pl
from jax.sharding import Mesh
from jax.sharding import PartitionSpec as P

NLON = 5120


def wave_tables(total_pairs, truncation):
    pair_ids = jnp.arange(total_pairs, dtype=jnp.int32)
    wavenumbers = jnp.stack([pair_ids, truncation - pair_ids], axis=1)
    flat = wavenumbers.reshape(-1)
    inner = 64
    outer = NLON // inner
    step = 2.0 * math.pi / NLON
    coarse = (flat[:, None] * (inner * jnp.arange(outer, dtype=jnp.int32))[None, :]) % NLON
    fine = (flat[:, None] * jnp.arange(inner, dtype=jnp.int32)[None, :]) % NLON
    coarse_angle = coarse.astype(jnp.float32) * step
    fine_angle = fine.astype(jnp.float32) * step
    cos_a = jnp.cos(coarse_angle)[:, :, None]
    sin_a = jnp.sin(coarse_angle)[:, :, None]
    cos_b = jnp.cos(fine_angle)[:, None, :]
    sin_b = jnp.sin(fine_angle)[:, None, :]
    rows = flat.shape[0]
    cosines = (cos_a * cos_b - sin_a * sin_b).reshape(rows, NLON).astype(jnp.bfloat16)
    sines = (sin_a * cos_b + cos_a * sin_b).reshape(rows, NLON).astype(jnp.bfloat16)
    table = lax.optimization_barrier(jnp.concatenate([cosines, sines], axis=0))
    return table, wavenumbers


def fourier_work(spectrum, row_counts, table, wavenumbers, truncation):
    pairs, lats, slots, channels = spectrum.shape
    kept_mask = (2 * wavenumbers[:, None, :] < row_counts[None, :, None]).astype(jnp.bfloat16)
    masked = spectrum * kept_mask[..., None]
    half_channels = channels // 2
    levels = half_channels // 2
    rows = lats * half_channels
    waves = pairs * slots
    flat = jnp.transpose(masked, (1, 3, 0, 2)).reshape(lats, channels, waves)
    real_part = flat[:, :half_channels].reshape(rows, waves)
    imag_part = flat[:, half_channels:].reshape(rows, waves)
    lhs = jnp.concatenate([real_part, -imag_part], axis=1)
    grid_values = jnp.dot(lhs, table, preferred_element_type=jnp.float32) * (
        1.0 / math.sqrt(truncation + 1)
    )
    grid_values = grid_values.reshape(lats, half_channels, NLON)
    vortex = grid_values[:, :levels]
    divergence = grid_values[:, levels:]
    products = jnp.concatenate(
        [vortex * divergence, 0.5 * (vortex * vortex - divergence * divergence)], axis=1
    ).astype(jnp.bfloat16)
    scale_back = 4.0 / math.sqrt(NLON)
    back = lax.dot_general(
        products.reshape(rows, NLON),
        table,
        (((1,), (1,)), ((), ())),
        preferred_element_type=jnp.float32,
    )
    real_out = back[:, :waves] * scale_back
    imag_out = back[:, waves:] * (-scale_back)
    out = jnp.concatenate(
        [real_out.reshape(lats, half_channels, waves), imag_out.reshape(lats, half_channels, waves)],
        axis=1,
    )
    out = jnp.transpose(out.reshape(lats, channels, pairs, slots), (2, 0, 3, 1))
    return (out * kept_mask[..., None].astype(jnp.float32)).astype(jnp.bfloat16)


def slot_codes(first_pair, pair_count, packed):
    pair_ids = first_pair + jnp.arange(pair_count, dtype=jnp.int32)
    positions = jnp.arange(packed, dtype=jnp.int32)
    boundary = packed - 1 - pair_ids
    in_second = (positions[None, :] >= boundary[:, None]).astype(jnp.int32)
    degree = positions[None, :] - in_second * boundary[:, None]
    return (2 * in_second + degree % 2).reshape(pair_count, 1, packed)


def inverse_kernel(leg_ref, spec_ref, code_ref, out_ref):
    block = leg_ref.shape[0]

    for pp in range(block):
        legendre_pair = leg_ref[pp]
        spectrum = spec_ref[:, pp, :]
        code = code_ref[pp]
        slot = code // 2
        sign = (1 - 2 * (code % 2)).astype(spectrum.dtype)
        zero = jnp.zeros_like(spectrum)
        first = jnp.where(slot == 0, spectrum, zero)
        second = jnp.where(slot == 1, spectrum, zero)
        masked = jnp.concatenate([first, second, first * sign, second * sign], axis=0)
        sums = lax.dot_general(
            legendre_pair, masked, (((1,), (1,)), ((), ())), preferred_element_type=jnp.float32
        )
        half = sums.shape[1] // 2
        out_ref[pp] = jnp.concatenate([sums[:, :half], sums[:, half:]], axis=0).astype(
            out_ref.dtype
        )


def direct_kernel(leg_ref, weight_ref, code_ref, out_ref):
    block = leg_ref.shape[0]
    channels = out_ref.shape[0]

    for pp in range(block):
        full = jnp.dot(weight_ref[pp], leg_ref[pp], preferred_element_type=jnp.float32)
        code = code_ref[pp]
        picked = jnp.where(code == 0, full[:channels], 0.0)
        for x in range(1, 4):
            picked = picked + jnp.where(code == x, full[x * channels : (x + 1) * channels], 0.0)
        out_ref[:, pp, :] = picked.astype(out_ref.dtype)


def legendre_inverse(legendre, spectrum, codes, block):
    pair_count, lat_count, packed = legendre.shape
    channels = spectrum.shape[0]
    return pl.pallas_call(
        inverse_kernel,
        grid=(pair_count // block,),
        in_specs=[
            pl.BlockSpec((block, lat_count, packed), lambda i: (i, 0, 0)),
            pl.BlockSpec((channels, block, packed), lambda i: (0, i, 0)),
            pl.BlockSpec((block, 1, packed), lambda i: (i, 0, 0)),
        ],
        out_specs=pl.BlockSpec((block, 2 * lat_count, 2 * channels), lambda i: (i, 0, 0)),
        out_shape=jax.ShapeDtypeStruct((pair_count, 2 * lat_count, 2 * channels), jnp.bfloat16),
    )(legendre, spectrum, codes)


def legendre_direct(legendre, weights, codes, block):
    pair_count, lat_count, packed = legendre.shape
    rows = weights.shape[1]
    channels = rows // 4
    return pl.pallas_call(
        direct_kernel,
        grid=(pair_count // block,),
        in_specs=[
            pl.BlockSpec((block, lat_count, packed), lambda i: (i, 0, 0)),
            pl.BlockSpec((block, rows, lat_count), lambda i: (i, 0, 0)),
            pl.BlockSpec((block, 1, packed), lambda i: (i, 0, 0)),
        ],
        out_specs=pl.BlockSpec((channels, block, packed), lambda i: (0, i, 0)),
        out_shape=jax.ShapeDtypeStruct((channels, pair_count, packed), jnp.bfloat16),
    )(legendre, weights, codes)


def local(spec_in, legendre, gauss_weights, row_points):
    pair_count, lat_count, packed = legendre.shape
    truncation = packed - 2
    groups = lax.axis_size("lat")
    cores = lax.axis_size("core")
    chips = lax.axis_size("chip")
    channels = spec_in.shape[0] * chips * cores
    block = math.gcd(pair_count, 8)
    first_pair = lax.axis_index("lat") * pair_count
    codes = slot_codes(first_pair, pair_count, packed)
    gathered = lax.all_gather(spec_in, "chip", axis=0, tiled=True)
    gathered = lax.all_gather(gathered, "core", axis=0, tiled=True)
    fourier = legendre_inverse(legendre, gathered, codes, block)
    fourier = fourier.reshape(pair_count, 2 * lat_count, 2, cores, chips)
    fourier = jnp.swapaxes(fourier, 3, 4).reshape(pair_count, 2 * lat_count, 2, channels)
    table, wavenumbers = wave_tables(pair_count * groups, truncation)
    local_rows = row_points.reshape(1, 2 * lat_count)
    band_lats = 2 * lat_count // groups
    lat_rows = lax.all_to_all(fourier, "lat", split_axis=1, concat_axis=0, tiled=True)
    my_rows = lax.dynamic_slice_in_dim(local_rows[0], lax.axis_index("lat") * band_lats, band_lats)
    answered = fourier_work(lat_rows, my_rows, table, wavenumbers, truncation)
    answered = answered.reshape(groups, pair_count, band_lats, 2, channels)
    returned = lax.all_to_all(answered, "lat", split_axis=0, concat_axis=0, tiled=True)
    back = jnp.moveaxis(returned, 0, 1).reshape(pair_count, 2 * lat_count, 2, channels)
    north_rows = back[:, :lat_count].astype(jnp.float32)
    south_rows = back[:, lat_count:].astype(jnp.float32)
    weights = gauss_weights[None, :, None, None]
    weighted = jnp.stack(
        [weights * (north_rows + south_rows), weights * (north_rows - south_rows)], axis=3
    )
    weighted = weighted.reshape(pair_count, lat_count, 4, chips, cores).astype(jnp.bfloat16)
    weighted = jnp.swapaxes(weighted, 3, 4).reshape(pair_count, lat_count, 4 * channels)
    weighted = jnp.swapaxes(weighted, 1, 2)
    partial = legendre_direct(legendre, weighted, codes, block)
    partial = lax.psum_scatter(partial, "core", scatter_dimension=0, tiled=True)
    return lax.psum_scatter(partial, "chip", scatter_dimension=0, tiled=True)


def solution(mesh):
    lat_size, lev_size = mesh.devices.shape
    cores = 2 if lev_size % 2 == 0 else 1
    inner = Mesh(mesh.devices.reshape(lat_size, lev_size // cores, cores), ("lat", "chip", "core"))
    lev = ("chip", "core")
    return jax.shard_map(
        local,
        mesh=inner,
        in_specs=(P(lev, "lat", None), P("lat", lev, None), P(lev), P(None, lev)),
        out_specs=P(lev, "lat", None),
        check_vma=False,
    )
```

```python
import math

import jax
import jax.numpy as jnp
from jax import lax
from jax.experimental import pallas as pl
from jax.sharding import PartitionSpec as P

NLON = 5120


def wave_tables(total_pairs, truncation):
    pair_ids = jnp.arange(total_pairs, dtype=jnp.int32)
    wavenumbers = jnp.stack([pair_ids, truncation - pair_ids], axis=1)
    flat = wavenumbers.reshape(-1)
    inner = 64
    outer = NLON // inner
    step = 2.0 * math.pi / NLON
    coarse = (flat[:, None] * (inner * jnp.arange(outer, dtype=jnp.int32))[None, :]) % NLON
    fine = (flat[:, None] * jnp.arange(inner, dtype=jnp.int32)[None, :]) % NLON
    coarse_angle = coarse.astype(jnp.float32) * step
    fine_angle = fine.astype(jnp.float32) * step
    cos_a = jnp.cos(coarse_angle)[:, :, None]
    sin_a = jnp.sin(coarse_angle)[:, :, None]
    cos_b = jnp.cos(fine_angle)[:, None, :]
    sin_b = jnp.sin(fine_angle)[:, None, :]
    rows = flat.shape[0]
    cosines = (cos_a * cos_b - sin_a * sin_b).reshape(rows, NLON).astype(jnp.bfloat16)
    sines = (sin_a * cos_b + cos_a * sin_b).reshape(rows, NLON).astype(jnp.bfloat16)
    table = lax.optimization_barrier(jnp.concatenate([cosines, -sines], axis=0))
    return table, wavenumbers


def fourier_work(spectrum, row_counts, table, wavenumbers, truncation):
    pairs, lats, slots, channels = spectrum.shape
    kept_mask = (2 * wavenumbers[:, None, :] < row_counts[None, :, None]).astype(jnp.bfloat16)
    masked = spectrum * kept_mask[..., None]
    half_channels = channels // 2
    levels = half_channels // 2
    rows = lats * half_channels
    waves = pairs * slots
    lhs = jnp.transpose(masked.reshape(pairs, lats, slots, 2, half_channels), (1, 4, 3, 0, 2))
    lhs = lhs.reshape(rows, 2 * waves)
    grid_values = jnp.dot(lhs, table, preferred_element_type=jnp.float32) * (
        1.0 / math.sqrt(truncation + 1)
    )
    grid_values = grid_values.reshape(lats, half_channels, NLON)
    vortex = grid_values[:, :levels]
    divergence = grid_values[:, levels:]
    products = jnp.concatenate(
        [vortex * divergence, 0.5 * (vortex * vortex - divergence * divergence)], axis=1
    ).astype(jnp.bfloat16)
    scale_back = 4.0 / math.sqrt(NLON)
    back = lax.dot_general(
        products.reshape(rows, NLON),
        table,
        (((1,), (1,)), ((), ())),
        preferred_element_type=jnp.float32,
    )
    keep = jnp.transpose(kept_mask, (1, 0, 2)).astype(jnp.float32) * scale_back
    back = back.reshape(lats, half_channels, 2, pairs, slots) * keep[:, None, None]
    out = jnp.transpose(back.astype(jnp.bfloat16), (3, 0, 4, 2, 1))
    return out.reshape(pairs, lats, slots, channels)


def slot_codes(first_pair, pair_count, packed):
    pair_ids = first_pair + jnp.arange(pair_count, dtype=jnp.int32)
    positions = jnp.arange(packed, dtype=jnp.int32)
    boundary = packed - 1 - pair_ids
    in_second = (positions[None, :] >= boundary[:, None]).astype(jnp.int32)
    degree = positions[None, :] - in_second * boundary[:, None]
    return (2 * in_second + degree % 2).reshape(pair_count, 1, packed)


def inverse_kernel(leg_ref, spec_ref, code_ref, out_ref):
    block = leg_ref.shape[0]

    for pp in range(block):
        legendre_pair = leg_ref[pp]
        spectrum = spec_ref[:, pp, :]
        code = code_ref[pp]
        slot = code // 2
        sign = (1 - 2 * (code % 2)).astype(spectrum.dtype)
        zero = jnp.zeros_like(spectrum)
        first = jnp.where(slot == 0, spectrum, zero)
        second = jnp.where(slot == 1, spectrum, zero)
        masked = jnp.concatenate([first, second, first * sign, second * sign], axis=0)
        sums = lax.dot_general(
            legendre_pair, masked, (((1,), (1,)), ((), ())), preferred_element_type=jnp.float32
        )
        half = sums.shape[1] // 2
        out_ref[pp] = jnp.concatenate([sums[:, :half], sums[:, half:]], axis=0).astype(
            out_ref.dtype
        )


def direct_kernel(leg_ref, weight_ref, code_ref, out_ref):
    block = leg_ref.shape[0]
    channels = out_ref.shape[0]

    for pp in range(block):
        full = jnp.dot(weight_ref[pp], leg_ref[pp], preferred_element_type=jnp.float32)
        code = code_ref[pp]
        picked = jnp.where(code == 0, full[:channels], 0.0)
        for x in range(1, 4):
            picked = picked + jnp.where(code == x, full[x * channels : (x + 1) * channels], 0.0)
        out_ref[:, pp, :] = picked.astype(out_ref.dtype)


def legendre_inverse(legendre, spectrum, codes, block):
    pair_count, lat_count, packed = legendre.shape
    channels = spectrum.shape[0]
    return pl.pallas_call(
        inverse_kernel,
        grid=(pair_count // block,),
        in_specs=[
            pl.BlockSpec((block, lat_count, packed), lambda i: (i, 0, 0)),
            pl.BlockSpec((channels, block, packed), lambda i: (0, i, 0)),
            pl.BlockSpec((block, 1, packed), lambda i: (i, 0, 0)),
        ],
        out_specs=pl.BlockSpec((block, 2 * lat_count, 2 * channels), lambda i: (i, 0, 0)),
        out_shape=jax.ShapeDtypeStruct((pair_count, 2 * lat_count, 2 * channels), jnp.bfloat16),
    )(legendre, spectrum, codes)


def legendre_direct(legendre, weights, codes, block):
    pair_count, lat_count, packed = legendre.shape
    rows = weights.shape[1]
    channels = rows // 4
    return pl.pallas_call(
        direct_kernel,
        grid=(pair_count // block,),
        in_specs=[
            pl.BlockSpec((block, lat_count, packed), lambda i: (i, 0, 0)),
            pl.BlockSpec((block, rows, lat_count), lambda i: (i, 0, 0)),
            pl.BlockSpec((block, 1, packed), lambda i: (i, 0, 0)),
        ],
        out_specs=pl.BlockSpec((channels, block, packed), lambda i: (0, i, 0)),
        out_shape=jax.ShapeDtypeStruct((channels, pair_count, packed), jnp.bfloat16),
    )(legendre, weights, codes)


def local(spec_in, legendre, gauss_weights, row_points):
    pair_count, lat_count, packed = legendre.shape
    truncation = packed - 2
    groups = lax.axis_size("lat")
    local_channels = spec_in.shape[0]
    channels = local_channels * lax.axis_size("lev")
    block = math.gcd(pair_count, 8)
    first_pair = lax.axis_index("lat") * pair_count
    codes = slot_codes(first_pair, pair_count, packed)
    gathered = lax.all_gather(spec_in, "lev", axis=0, tiled=True)
    fourier = legendre_inverse(legendre, gathered, codes, block)
    fourier = fourier.reshape(pair_count, 2 * lat_count, 2, channels)
    table, wavenumbers = wave_tables(pair_count * groups, truncation)
    local_rows = row_points.reshape(1, 2 * lat_count)
    band_lats = 2 * lat_count // groups
    lat_rows = lax.all_to_all(fourier, "lat", split_axis=1, concat_axis=0, tiled=True)
    my_rows = lax.dynamic_slice_in_dim(local_rows[0], lax.axis_index("lat") * band_lats, band_lats)
    answered = fourier_work(lat_rows, my_rows, table, wavenumbers, truncation)
    answered = answered.reshape(groups, pair_count, band_lats, 2, channels)
    returned = lax.all_to_all(answered, "lat", split_axis=0, concat_axis=0, tiled=True)
    back = jnp.moveaxis(returned, 0, 1).reshape(pair_count, 2 * lat_count, 2, channels)
    north_rows = back[:, :lat_count].astype(jnp.float32)
    south_rows = back[:, lat_count:].astype(jnp.float32)
    weights = gauss_weights[None, :, None, None]
    weighted = jnp.stack(
        [weights * (north_rows + south_rows), weights * (north_rows - south_rows)], axis=3
    )
    weighted = weighted.reshape(pair_count, lat_count, 4 * channels).astype(jnp.bfloat16)
    weighted = jnp.swapaxes(weighted, 1, 2)
    partial = legendre_direct(legendre, weighted, codes, block)
    return lax.psum_scatter(partial, "lev", scatter_dimension=0, tiled=True)


def solution(mesh):
    return jax.shard_map(
        local,
        mesh=mesh,
        in_specs=(P("lev", "lat", None), P("lat", "lev", None), P("lev"), P(None, "lev")),
        out_specs=P("lev", "lat", None),
        check_vma=False,
    )
```

```python
import math

import jax
import jax.numpy as jnp
from jax import lax
from jax.experimental import pallas as pl
from jax.sharding import PartitionSpec as P

NLON = 5120


def wave_tables(total_pairs, truncation):
    pair_ids = jnp.arange(total_pairs, dtype=jnp.int32)
    wavenumbers = jnp.stack([pair_ids, truncation - pair_ids], axis=1)
    flat = wavenumbers.reshape(-1)
    inner = 64
    outer = NLON // inner
    step = 2.0 * math.pi / NLON
    coarse = (flat[:, None] * (inner * jnp.arange(outer, dtype=jnp.int32))[None, :]) % NLON
    fine = (flat[:, None] * jnp.arange(inner, dtype=jnp.int32)[None, :]) % NLON
    coarse_angle = coarse.astype(jnp.float32) * step
    fine_angle = fine.astype(jnp.float32) * step
    cos_a = jnp.cos(coarse_angle)[:, :, None]
    sin_a = jnp.sin(coarse_angle)[:, :, None]
    cos_b = jnp.cos(fine_angle)[:, None, :]
    sin_b = jnp.sin(fine_angle)[:, None, :]
    rows = flat.shape[0]
    cosines = (cos_a * cos_b - sin_a * sin_b).reshape(rows, NLON).astype(jnp.bfloat16)
    sines = (sin_a * cos_b + cos_a * sin_b).reshape(rows, NLON).astype(jnp.bfloat16)
    table = lax.optimization_barrier(jnp.concatenate([cosines, sines], axis=0))
    return table, wavenumbers


def fourier_work(spectrum, row_counts, table, wavenumbers, truncation):
    pairs, lats, slots, channels = spectrum.shape
    kept_mask = (2 * wavenumbers[:, None, :] < row_counts[None, :, None]).astype(jnp.bfloat16)
    masked = spectrum * kept_mask[..., None]
    half_channels = channels // 2
    levels = half_channels // 2
    rows = lats * half_channels
    waves = pairs * slots
    flat = jnp.transpose(masked, (1, 3, 0, 2)).reshape(lats, channels, waves)
    real_part = flat[:, :half_channels].reshape(rows, waves)
    imag_part = flat[:, half_channels:].reshape(rows, waves)
    lhs = jnp.concatenate([real_part, -imag_part], axis=1)
    grid_values = jnp.dot(lhs, table, preferred_element_type=jnp.float32) * (
        1.0 / math.sqrt(truncation + 1)
    )
    grid_values = grid_values.reshape(lats, half_channels, NLON)
    vortex = grid_values[:, :levels]
    divergence = grid_values[:, levels:]
    products = jnp.concatenate(
        [vortex * divergence, 0.5 * (vortex * vortex - divergence * divergence)], axis=1
    ).astype(jnp.bfloat16)
    scale_back = 4.0 / math.sqrt(NLON)
    back = lax.dot_general(
        products.reshape(rows, NLON),
        table,
        (((1,), (1,)), ((), ())),
        preferred_element_type=jnp.float32,
    )
    sign = jnp.where(jnp.arange(2) == 0, scale_back, -scale_back).astype(jnp.float32)
    keep = jnp.transpose(kept_mask, (1, 0, 2)).astype(jnp.float32).reshape(lats, 1, 1, waves)
    back = lax.optimization_barrier(back).reshape(lats, half_channels, 2, waves) * sign[:, None] * keep
    out = jnp.transpose(back.astype(jnp.bfloat16).reshape(lats, half_channels, 2, pairs, slots), (3, 0, 4, 2, 1))
    return out.reshape(pairs, lats, slots, channels)


def slot_codes(first_pair, pair_count, packed):
    pair_ids = first_pair + jnp.arange(pair_count, dtype=jnp.int32)
    positions = jnp.arange(packed, dtype=jnp.int32)
    boundary = packed - 1 - pair_ids
    in_second = (positions[None, :] >= boundary[:, None]).astype(jnp.int32)
    degree = positions[None, :] - in_second * boundary[:, None]
    return (2 * in_second + degree % 2).reshape(pair_count, 1, packed)


def inverse_kernel(leg_ref, spec_ref, code_ref, out_ref):
    block = leg_ref.shape[0]

    for pp in range(block):
        legendre_pair = leg_ref[pp]
        spectrum = spec_ref[:, pp, :]
        code = code_ref[pp]
        slot = code // 2
        sign = (1 - 2 * (code % 2)).astype(spectrum.dtype)
        zero = jnp.zeros_like(spectrum)
        first = jnp.where(slot == 0, spectrum, zero)
        second = jnp.where(slot == 1, spectrum, zero)
        masked = jnp.concatenate([first, second, first * sign, second * sign], axis=0)
        sums = lax.dot_general(
            legendre_pair, masked, (((1,), (1,)), ((), ())), preferred_element_type=jnp.float32
        )
        half = sums.shape[1] // 2
        out_ref[pp] = jnp.concatenate([sums[:, :half], sums[:, half:]], axis=0).astype(
            out_ref.dtype
        )


def direct_kernel(leg_ref, weight_ref, code_ref, out_ref):
    block = leg_ref.shape[0]
    channels = out_ref.shape[0]

    for pp in range(block):
        full = jnp.dot(weight_ref[pp], leg_ref[pp], preferred_element_type=jnp.float32)
        code = code_ref[pp]
        picked = jnp.where(code == 0, full[:channels], 0.0)
        for x in range(1, 4):
            picked = picked + jnp.where(code == x, full[x * channels : (x + 1) * channels], 0.0)
        out_ref[:, pp, :] = picked.astype(out_ref.dtype)


def legendre_inverse(legendre, spectrum, codes, block):
    pair_count, lat_count, packed = legendre.shape
    channels = spectrum.shape[0]
    return pl.pallas_call(
        inverse_kernel,
        grid=(pair_count // block,),
        in_specs=[
            pl.BlockSpec((block, lat_count, packed), lambda i: (i, 0, 0)),
            pl.BlockSpec((channels, block, packed), lambda i: (0, i, 0)),
            pl.BlockSpec((block, 1, packed), lambda i: (i, 0, 0)),
        ],
        out_specs=pl.BlockSpec((block, 2 * lat_count, 2 * channels), lambda i: (i, 0, 0)),
        out_shape=jax.ShapeDtypeStruct((pair_count, 2 * lat_count, 2 * channels), jnp.bfloat16),
    )(legendre, spectrum, codes)


def legendre_direct(legendre, weights, codes, block):
    pair_count, lat_count, packed = legendre.shape
    rows = weights.shape[1]
    channels = rows // 4
    return pl.pallas_call(
        direct_kernel,
        grid=(pair_count // block,),
        in_specs=[
            pl.BlockSpec((block, lat_count, packed), lambda i: (i, 0, 0)),
            pl.BlockSpec((block, rows, lat_count), lambda i: (i, 0, 0)),
            pl.BlockSpec((block, 1, packed), lambda i: (i, 0, 0)),
        ],
        out_specs=pl.BlockSpec((channels, block, packed), lambda i: (0, i, 0)),
        out_shape=jax.ShapeDtypeStruct((channels, pair_count, packed), jnp.bfloat16),
    )(legendre, weights, codes)


def local(spec_in, legendre, gauss_weights, row_points):
    pair_count, lat_count, packed = legendre.shape
    truncation = packed - 2
    groups = lax.axis_size("lat")
    local_channels = spec_in.shape[0]
    channels = local_channels * lax.axis_size("lev")
    block = math.gcd(pair_count, 8)
    first_pair = lax.axis_index("lat") * pair_count
    codes = slot_codes(first_pair, pair_count, packed)
    gathered = lax.all_gather(spec_in, "lev", axis=0, tiled=True)
    fourier = legendre_inverse(legendre, gathered, codes, block)
    fourier = fourier.reshape(pair_count, 2 * lat_count, 2, channels)
    table, wavenumbers = wave_tables(pair_count * groups, truncation)
    local_rows = row_points.reshape(1, 2 * lat_count)
    band_lats = 2 * lat_count // groups
    lat_rows = lax.all_to_all(fourier, "lat", split_axis=1, concat_axis=0, tiled=True)
    my_rows = lax.dynamic_slice_in_dim(local_rows[0], lax.axis_index("lat") * band_lats, band_lats)
    answered = fourier_work(lat_rows, my_rows, table, wavenumbers, truncation)
    answered = answered.reshape(groups, pair_count, band_lats, 2, channels)
    returned = lax.all_to_all(answered, "lat", split_axis=0, concat_axis=0, tiled=True)
    back = jnp.moveaxis(returned, 0, 1).reshape(pair_count, 2 * lat_count, 2, channels)
    north_rows = back[:, :lat_count].astype(jnp.float32)
    south_rows = back[:, lat_count:].astype(jnp.float32)
    weights = gauss_weights[None, :, None, None]
    weighted = jnp.stack(
        [weights * (north_rows + south_rows), weights * (north_rows - south_rows)], axis=3
    )
    weighted = weighted.reshape(pair_count, lat_count, 4 * channels).astype(jnp.bfloat16)
    weighted = jnp.swapaxes(weighted, 1, 2)
    partial = legendre_direct(legendre, weighted, codes, block)
    return lax.psum_scatter(partial, "lev", scatter_dimension=0, tiled=True)


def solution(mesh):
    return jax.shard_map(
        local,
        mesh=mesh,
        in_specs=(P("lev", "lat", None), P("lat", "lev", None), P("lev"), P(None, "lev")),
        out_specs=P("lev", "lat", None),
        check_vma=False,
    )
```

```python
import math

import jax
import jax.numpy as jnp
from jax import lax
from jax.experimental import pallas as pl
from jax.sharding import PartitionSpec as P

NLON = 5120


def wave_tables(total_pairs, truncation):
    pair_ids = jnp.arange(total_pairs, dtype=jnp.int32)
    wavenumbers = jnp.stack([pair_ids, truncation - pair_ids], axis=1)
    flat = wavenumbers.reshape(-1)
    inner = 64
    outer = NLON // inner
    step = 2.0 * math.pi / NLON
    coarse = (flat[:, None] * (inner * jnp.arange(outer, dtype=jnp.int32))[None, :]) % NLON
    fine = (flat[:, None] * jnp.arange(inner, dtype=jnp.int32)[None, :]) % NLON
    coarse_angle = coarse.astype(jnp.float32) * step
    fine_angle = fine.astype(jnp.float32) * step
    cos_a = jnp.cos(coarse_angle)[:, :, None]
    sin_a = jnp.sin(coarse_angle)[:, :, None]
    cos_b = jnp.cos(fine_angle)[:, None, :]
    sin_b = jnp.sin(fine_angle)[:, None, :]
    rows = flat.shape[0]
    cosines = (cos_a * cos_b - sin_a * sin_b).reshape(rows, NLON).astype(jnp.bfloat16)
    sines = (sin_a * cos_b + cos_a * sin_b).reshape(rows, NLON).astype(jnp.bfloat16)
    table = lax.optimization_barrier(jnp.concatenate([cosines, sines], axis=0))
    return table, wavenumbers


def fourier_work(spectrum, row_counts, table, wavenumbers, truncation):
    pairs, lats, slots, channels = spectrum.shape
    kept_mask = (2 * wavenumbers[:, None, :] < row_counts[None, :, None]).astype(jnp.bfloat16)
    masked = spectrum * kept_mask[..., None]
    half_channels = channels // 2
    levels = half_channels // 2
    rows = lats * half_channels
    waves = pairs * slots
    flat = jnp.transpose(masked, (1, 3, 0, 2)).reshape(lats, channels, waves)
    real_part = flat[:, :half_channels].reshape(rows, waves)
    imag_part = flat[:, half_channels:].reshape(rows, waves)
    lhs = jnp.concatenate([real_part, -imag_part], axis=1)
    grid_values = jnp.dot(lhs, table, preferred_element_type=jnp.float32) * (
        1.0 / math.sqrt(truncation + 1)
    )
    grid_values = grid_values.reshape(lats, half_channels, NLON)
    vortex = grid_values[:, :levels]
    divergence = grid_values[:, levels:]
    products = jnp.concatenate(
        [vortex * divergence, 0.5 * (vortex * vortex - divergence * divergence)], axis=1
    ).astype(jnp.bfloat16)
    scale_back = 4.0 / math.sqrt(NLON)
    back = lax.dot_general(
        products.reshape(rows, NLON),
        table,
        (((1,), (1,)), ((), ())),
        preferred_element_type=jnp.float32,
    )
    real_out = back[:, :waves] * scale_back
    imag_out = back[:, waves:] * (-scale_back)
    out = jnp.concatenate(
        [real_out.reshape(lats, half_channels, waves), imag_out.reshape(lats, half_channels, waves)],
        axis=1,
    )
    out = jnp.transpose(out.reshape(lats, channels, pairs, slots), (2, 0, 3, 1))
    return (out * kept_mask[..., None].astype(jnp.float32)).astype(jnp.bfloat16)


def slot_codes(first_pair, pair_count, packed):
    pair_ids = first_pair + jnp.arange(pair_count, dtype=jnp.int32)
    positions = jnp.arange(packed, dtype=jnp.int32)
    boundary = packed - 1 - pair_ids
    in_second = (positions[None, :] >= boundary[:, None]).astype(jnp.int32)
    degree = positions[None, :] - in_second * boundary[:, None]
    return (2 * in_second + degree % 2).reshape(pair_count, 1, packed)


def inverse_kernel(leg_ref, spec_ref, code_ref, out_ref):
    block = leg_ref.shape[0]

    for pp in range(block):
        legendre_pair = leg_ref[pp]
        spectrum = spec_ref[:, pp, :]
        code = code_ref[pp]
        slot = code // 2
        sign = (1 - 2 * (code % 2)).astype(spectrum.dtype)
        zero = jnp.zeros_like(spectrum)
        first = jnp.where(slot == 0, spectrum, zero)
        second = jnp.where(slot == 1, spectrum, zero)
        masked = jnp.concatenate([first, second, first * sign, second * sign], axis=0)
        sums = lax.dot_general(
            legendre_pair, masked, (((1,), (1,)), ((), ())), preferred_element_type=jnp.float32
        )
        half = sums.shape[1] // 2
        out_ref[pp] = jnp.concatenate([sums[:, :half], sums[:, half:]], axis=0).astype(
            out_ref.dtype
        )


def direct_kernel(leg_ref, weight_ref, code_ref, out_ref):
    block = leg_ref.shape[0]
    channels = out_ref.shape[0]

    for pp in range(block):
        full = jnp.dot(weight_ref[pp], leg_ref[pp], preferred_element_type=jnp.float32)
        code = code_ref[pp]
        picked = jnp.where(code == 0, full[:channels], 0.0)
        for x in range(1, 4):
            picked = picked + jnp.where(code == x, full[x * channels : (x + 1) * channels], 0.0)
        out_ref[:, pp, :] = picked.astype(out_ref.dtype)


def legendre_inverse(legendre, spectrum, codes, block):
    pair_count, lat_count, packed = legendre.shape
    channels = spectrum.shape[0]
    return pl.pallas_call(
        inverse_kernel,
        grid=(pair_count // block,),
        in_specs=[
            pl.BlockSpec((block, lat_count, packed), lambda i: (i, 0, 0)),
            pl.BlockSpec((channels, block, packed), lambda i: (0, i, 0)),
            pl.BlockSpec((block, 1, packed), lambda i: (i, 0, 0)),
        ],
        out_specs=pl.BlockSpec((block, 2 * lat_count, 2 * channels), lambda i: (i, 0, 0)),
        out_shape=jax.ShapeDtypeStruct((pair_count, 2 * lat_count, 2 * channels), jnp.bfloat16),
    )(legendre, spectrum, codes)


def legendre_direct(legendre, weights, codes, block):
    pair_count, lat_count, packed = legendre.shape
    rows = weights.shape[1]
    channels = rows // 4
    return pl.pallas_call(
        direct_kernel,
        grid=(pair_count // block,),
        in_specs=[
            pl.BlockSpec((block, lat_count, packed), lambda i: (i, 0, 0)),
            pl.BlockSpec((block, rows, lat_count), lambda i: (i, 0, 0)),
            pl.BlockSpec((block, 1, packed), lambda i: (i, 0, 0)),
        ],
        out_specs=pl.BlockSpec((channels, block, packed), lambda i: (0, i, 0)),
        out_shape=jax.ShapeDtypeStruct((channels, pair_count, packed), jnp.bfloat16),
    )(legendre, weights, codes)


def local(spec_in, legendre, gauss_weights, row_points):
    pair_count, lat_count, packed = legendre.shape
    truncation = packed - 2
    groups = lax.axis_size("lat")
    local_channels = spec_in.shape[0]
    channels = local_channels * lax.axis_size("lev")
    block = math.gcd(pair_count, 8)
    first_pair = lax.axis_index("lat") * pair_count
    codes = slot_codes(first_pair, pair_count, packed)
    gathered = lax.all_gather(spec_in, "lev", axis=0, tiled=True)
    table, wavenumbers = wave_tables(pair_count * groups, truncation)
    gathered, table = lax.optimization_barrier((gathered, table))
    fourier = legendre_inverse(legendre, gathered, codes, block)
    fourier = fourier.reshape(pair_count, 2 * lat_count, 2, channels)
    local_rows = row_points.reshape(1, 2 * lat_count)
    band_lats = 2 * lat_count // groups
    lat_rows = lax.all_to_all(fourier, "lat", split_axis=1, concat_axis=0, tiled=True)
    my_rows = lax.dynamic_slice_in_dim(local_rows[0], lax.axis_index("lat") * band_lats, band_lats)
    answered = fourier_work(lat_rows, my_rows, table, wavenumbers, truncation)
    answered = answered.reshape(groups, pair_count, band_lats, 2, channels)
    returned = lax.all_to_all(answered, "lat", split_axis=0, concat_axis=0, tiled=True)
    back = jnp.moveaxis(returned, 0, 1).reshape(pair_count, 2 * lat_count, 2, channels)
    north_rows = back[:, :lat_count].astype(jnp.float32)
    south_rows = back[:, lat_count:].astype(jnp.float32)
    weights = gauss_weights[None, :, None, None]
    weighted = jnp.stack(
        [weights * (north_rows + south_rows), weights * (north_rows - south_rows)], axis=3
    )
    weighted = weighted.reshape(pair_count, lat_count, 4 * channels).astype(jnp.bfloat16)
    weighted = jnp.swapaxes(weighted, 1, 2)
    partial = legendre_direct(legendre, weighted, codes, block)
    return lax.psum_scatter(partial, "lev", scatter_dimension=0, tiled=True)


def solution(mesh):
    return jax.shard_map(
        local,
        mesh=mesh,
        in_specs=(P("lev", "lat", None), P("lat", "lev", None), P("lev"), P(None, "lev")),
        out_specs=P("lev", "lat", None),
        check_vma=False,
    )
```

```python
import math

import jax
import jax.numpy as jnp
from jax import lax
from jax.experimental import pallas as pl
from jax.sharding import PartitionSpec as P

NLON = 5120


def wave_tables(total_pairs, truncation):
    pair_ids = jnp.arange(total_pairs, dtype=jnp.int32)
    wavenumbers = jnp.stack([pair_ids, truncation - pair_ids], axis=1)
    flat = wavenumbers.reshape(-1)
    inner = 64
    outer = NLON // inner
    step = 2.0 * math.pi / NLON
    coarse = (flat[:, None] * (inner * jnp.arange(outer, dtype=jnp.int32))[None, :]) % NLON
    fine = (flat[:, None] * jnp.arange(inner, dtype=jnp.int32)[None, :]) % NLON
    coarse_angle = coarse.astype(jnp.float32) * step
    fine_angle = fine.astype(jnp.float32) * step
    cos_a = jnp.cos(coarse_angle)[:, :, None]
    sin_a = jnp.sin(coarse_angle)[:, :, None]
    cos_b = jnp.cos(fine_angle)[:, None, :]
    sin_b = jnp.sin(fine_angle)[:, None, :]
    rows = flat.shape[0]
    cosines = (cos_a * cos_b - sin_a * sin_b).reshape(rows, NLON).astype(jnp.bfloat16)
    sines = (sin_a * cos_b + cos_a * sin_b).reshape(rows, NLON).astype(jnp.bfloat16)
    table = lax.optimization_barrier(jnp.concatenate([cosines, sines], axis=0))
    return table, wavenumbers


def fourier_work(spectrum, row_counts, table, wavenumbers, truncation):
    pairs, lats, slots, channels = spectrum.shape
    kept_mask = (2 * wavenumbers[:, None, :] < row_counts[None, :, None]).astype(jnp.bfloat16)
    masked = spectrum * kept_mask[..., None]
    half_channels = channels // 2
    levels = half_channels // 2
    rows = lats * half_channels
    waves = pairs * slots
    flat = jnp.transpose(masked, (1, 3, 0, 2)).reshape(lats, channels, waves)
    real_part = flat[:, :half_channels].reshape(rows, waves)
    imag_part = flat[:, half_channels:].reshape(rows, waves)
    lhs = jnp.concatenate([real_part, -imag_part], axis=1)
    grid_values = jnp.dot(lhs, table, preferred_element_type=jnp.float32) * (
        1.0 / math.sqrt(truncation + 1)
    )
    grid_values = grid_values.reshape(lats, half_channels, NLON)
    vortex = grid_values[:, :levels]
    divergence = grid_values[:, levels:]
    products = jnp.concatenate(
        [vortex * divergence, 0.5 * (vortex * vortex - divergence * divergence)], axis=1
    ).astype(jnp.bfloat16)
    scale_back = 4.0 / math.sqrt(NLON)
    back = lax.dot_general(
        products.reshape(rows, NLON),
        table,
        (((1,), (1,)), ((), ())),
        preferred_element_type=jnp.float32,
    )
    real_out = back[:, :waves] * scale_back
    imag_out = back[:, waves:] * (-scale_back)
    out = jnp.concatenate(
        [real_out.reshape(lats, half_channels, waves), imag_out.reshape(lats, half_channels, waves)],
        axis=1,
    )
    out = jnp.transpose(out.reshape(lats, channels, pairs, slots), (2, 0, 3, 1))
    return (out * kept_mask[..., None].astype(jnp.float32)).astype(jnp.bfloat16)


def exchange(pieces, axis):
    count = pieces.shape[0]
    me = lax.axis_index(axis)
    result = pieces
    for shift in range(count):
        part = lax.dynamic_index_in_dim(pieces, (me + shift) % count, axis=0)
        if shift:
            part = lax.ppermute(part, axis, [(j, (j + shift) % count) for j in range(count)])
        result = lax.dynamic_update_index_in_dim(result, part, (me - shift) % count, 0)
    return result


def slot_codes(first_pair, pair_count, packed):
    pair_ids = first_pair + jnp.arange(pair_count, dtype=jnp.int32)
    positions = jnp.arange(packed, dtype=jnp.int32)
    boundary = packed - 1 - pair_ids
    in_second = (positions[None, :] >= boundary[:, None]).astype(jnp.int32)
    degree = positions[None, :] - in_second * boundary[:, None]
    return (2 * in_second + degree % 2).reshape(pair_count, 1, packed)


def inverse_kernel(leg_ref, spec_ref, code_ref, out_ref):
    block = leg_ref.shape[0]

    for pp in range(block):
        legendre_pair = leg_ref[pp]
        spectrum = spec_ref[:, pp, :]
        code = code_ref[pp]
        slot = code // 2
        sign = (1 - 2 * (code % 2)).astype(spectrum.dtype)
        zero = jnp.zeros_like(spectrum)
        first = jnp.where(slot == 0, spectrum, zero)
        second = jnp.where(slot == 1, spectrum, zero)
        masked = jnp.concatenate([first, second, first * sign, second * sign], axis=0)
        sums = lax.dot_general(
            legendre_pair, masked, (((1,), (1,)), ((), ())), preferred_element_type=jnp.float32
        )
        half = sums.shape[1] // 2
        out_ref[pp] = jnp.concatenate([sums[:, :half], sums[:, half:]], axis=0).astype(
            out_ref.dtype
        )


def direct_kernel(leg_ref, weight_ref, code_ref, out_ref):
    block = leg_ref.shape[0]
    channels = out_ref.shape[0]

    for pp in range(block):
        full = jnp.dot(weight_ref[pp], leg_ref[pp], preferred_element_type=jnp.float32)
        code = code_ref[pp]
        picked = jnp.where(code == 0, full[:channels], 0.0)
        for x in range(1, 4):
            picked = picked + jnp.where(code == x, full[x * channels : (x + 1) * channels], 0.0)
        out_ref[:, pp, :] = picked.astype(out_ref.dtype)


def legendre_inverse(legendre, spectrum, codes, block):
    pair_count, lat_count, packed = legendre.shape
    channels = spectrum.shape[0]
    return pl.pallas_call(
        inverse_kernel,
        grid=(pair_count // block,),
        in_specs=[
            pl.BlockSpec((block, lat_count, packed), lambda i: (i, 0, 0)),
            pl.BlockSpec((channels, block, packed), lambda i: (0, i, 0)),
            pl.BlockSpec((block, 1, packed), lambda i: (i, 0, 0)),
        ],
        out_specs=pl.BlockSpec((block, 2 * lat_count, 2 * channels), lambda i: (i, 0, 0)),
        out_shape=jax.ShapeDtypeStruct((pair_count, 2 * lat_count, 2 * channels), jnp.bfloat16),
    )(legendre, spectrum, codes)


def legendre_direct(legendre, weights, codes, block):
    pair_count, lat_count, packed = legendre.shape
    rows = weights.shape[1]
    channels = rows // 4
    return pl.pallas_call(
        direct_kernel,
        grid=(pair_count // block,),
        in_specs=[
            pl.BlockSpec((block, lat_count, packed), lambda i: (i, 0, 0)),
            pl.BlockSpec((block, rows, lat_count), lambda i: (i, 0, 0)),
            pl.BlockSpec((block, 1, packed), lambda i: (i, 0, 0)),
        ],
        out_specs=pl.BlockSpec((channels, block, packed), lambda i: (0, i, 0)),
        out_shape=jax.ShapeDtypeStruct((channels, pair_count, packed), jnp.bfloat16),
    )(legendre, weights, codes)


def local(spec_in, legendre, gauss_weights, row_points):
    pair_count, lat_count, packed = legendre.shape
    truncation = packed - 2
    groups = lax.axis_size("lat")
    local_channels = spec_in.shape[0]
    channels = local_channels * lax.axis_size("lev")
    block = math.gcd(pair_count, 8)
    first_pair = lax.axis_index("lat") * pair_count
    codes = slot_codes(first_pair, pair_count, packed)
    gathered = lax.all_gather(spec_in, "lev", axis=0, tiled=True)
    table, wavenumbers = wave_tables(pair_count * groups, truncation)
    gathered, table = lax.optimization_barrier((gathered, table))
    fourier = legendre_inverse(legendre, gathered, codes, block)
    fourier = fourier.reshape(pair_count, 2 * lat_count, 2, channels)
    local_rows = row_points.reshape(1, 2 * lat_count)
    band_lats = 2 * lat_count // groups
    outgoing = jnp.moveaxis(fourier.reshape(pair_count, groups, band_lats, 2, channels), 1, 0)
    lat_rows = exchange(outgoing, "lat").reshape(groups * pair_count, band_lats, 2, channels)
    my_rows = lax.dynamic_slice_in_dim(local_rows[0], lax.axis_index("lat") * band_lats, band_lats)
    answered = fourier_work(lat_rows, my_rows, table, wavenumbers, truncation)
    answered = answered.reshape(groups, pair_count, band_lats, 2, channels)
    returned = exchange(answered, "lat")
    back = jnp.moveaxis(returned, 0, 1).reshape(pair_count, 2 * lat_count, 2, channels)
    north_rows = back[:, :lat_count].astype(jnp.float32)
    south_rows = back[:, lat_count:].astype(jnp.float32)
    weights = gauss_weights[None, :, None, None]
    weighted = jnp.stack(
        [weights * (north_rows + south_rows), weights * (north_rows - south_rows)], axis=3
    )
    weighted = weighted.reshape(pair_count, lat_count, 4 * channels).astype(jnp.bfloat16)
    weighted = jnp.swapaxes(weighted, 1, 2)
    partial = legendre_direct(legendre, weighted, codes, block)
    return lax.psum_scatter(partial, "lev", scatter_dimension=0, tiled=True)


def solution(mesh):
    return jax.shard_map(
        local,
        mesh=mesh,
        in_specs=(P("lev", "lat", None), P("lat", "lev", None), P("lev"), P(None, "lev")),
        out_specs=P("lev", "lat", None),
        check_vma=False,
    )
```

```python
import math

import jax
import jax.numpy as jnp
from jax import lax
from jax.experimental import pallas as pl
from jax.sharding import PartitionSpec as P

NLON = 5120


def wave_tables(total_pairs, truncation):
    pair_ids = jnp.arange(total_pairs, dtype=jnp.int32)
    wavenumbers = jnp.stack([pair_ids, truncation - pair_ids], axis=1)
    flat = wavenumbers.reshape(-1)
    inner = 64
    outer = NLON // inner
    step = 2.0 * math.pi / NLON
    coarse = (flat[:, None] * (inner * jnp.arange(outer, dtype=jnp.int32))[None, :]) % NLON
    fine = (flat[:, None] * jnp.arange(inner, dtype=jnp.int32)[None, :]) % NLON
    coarse_angle = coarse.astype(jnp.float32) * step
    fine_angle = fine.astype(jnp.float32) * step
    cos_a = jnp.cos(coarse_angle)[:, :, None]
    sin_a = jnp.sin(coarse_angle)[:, :, None]
    cos_b = jnp.cos(fine_angle)[:, None, :]
    sin_b = jnp.sin(fine_angle)[:, None, :]
    rows = flat.shape[0]
    cosines = (cos_a * cos_b - sin_a * sin_b).reshape(rows, NLON).astype(jnp.bfloat16)
    sines = (sin_a * cos_b + cos_a * sin_b).reshape(rows, NLON).astype(jnp.bfloat16)
    table = lax.optimization_barrier(jnp.concatenate([cosines, sines], axis=0))
    return table, wavenumbers


def fourier_work(spectrum, row_counts, table, wavenumbers, truncation):
    pairs, lats, slots, channels = spectrum.shape
    kept_mask = (2 * wavenumbers[:, None, :] < row_counts[None, :, None]).astype(jnp.bfloat16)
    masked = spectrum * kept_mask[..., None]
    half_channels = channels // 2
    levels = half_channels // 2
    rows = lats * half_channels
    waves = pairs * slots
    flat = jnp.transpose(masked, (1, 3, 0, 2)).reshape(lats, channels, waves)
    real_part = flat[:, :half_channels].reshape(rows, waves)
    imag_part = flat[:, half_channels:].reshape(rows, waves)
    lhs = jnp.concatenate([real_part, imag_part], axis=1)
    grid_values = jnp.dot(lhs, table, preferred_element_type=jnp.float32) * (
        1.0 / math.sqrt(truncation + 1)
    )
    grid_values = grid_values.reshape(lats, half_channels, NLON)
    vortex = grid_values[:, :levels]
    divergence = grid_values[:, levels:]
    products = jnp.concatenate(
        [vortex * divergence, 0.5 * (vortex * vortex - divergence * divergence)], axis=1
    ).astype(jnp.bfloat16)
    scale_back = 4.0 / math.sqrt(NLON)
    back = lax.dot_general(
        products.reshape(rows, NLON),
        table,
        (((1,), (1,)), ((), ())),
        preferred_element_type=jnp.float32,
    )
    real_out = back[:, :waves] * scale_back
    imag_out = back[:, waves:] * (-scale_back)
    out = jnp.concatenate(
        [real_out.reshape(lats, half_channels, waves), imag_out.reshape(lats, half_channels, waves)],
        axis=1,
    )
    out = jnp.transpose(out.reshape(lats, channels, pairs, slots), (2, 0, 3, 1))
    return (out * kept_mask[..., None].astype(jnp.float32)).astype(jnp.bfloat16)


def slot_codes(first_pair, pair_count, packed):
    pair_ids = first_pair + jnp.arange(pair_count, dtype=jnp.int32)
    positions = jnp.arange(packed, dtype=jnp.int32)
    boundary = packed - 1 - pair_ids
    in_second = (positions[None, :] >= boundary[:, None]).astype(jnp.int32)
    degree = positions[None, :] - in_second * boundary[:, None]
    return (2 * in_second + degree % 2).reshape(pair_count, 1, packed)


def inverse_kernel(leg_ref, spec_ref, code_ref, out_ref):
    block = leg_ref.shape[0]

    for pp in range(block):
        legendre_pair = leg_ref[pp]
        spectrum = spec_ref[:, pp, :]
        rows = lax.broadcasted_iota(jnp.int32, spectrum.shape, 0)
        spectrum = jnp.where(rows < spectrum.shape[0] // 2, spectrum, -spectrum)
        code = code_ref[pp]
        slot = code // 2
        sign = (1 - 2 * (code % 2)).astype(spectrum.dtype)
        zero = jnp.zeros_like(spectrum)
        first = jnp.where(slot == 0, spectrum, zero)
        second = jnp.where(slot == 1, spectrum, zero)
        masked = jnp.concatenate([first, second, first * sign, second * sign], axis=0)
        sums = lax.dot_general(
            legendre_pair, masked, (((1,), (1,)), ((), ())), preferred_element_type=jnp.float32
        )
        half = sums.shape[1] // 2
        out_ref[pp] = jnp.concatenate([sums[:, :half], sums[:, half:]], axis=0).astype(
            out_ref.dtype
        )


def direct_kernel(leg_ref, weight_ref, code_ref, out_ref):
    block = leg_ref.shape[0]
    channels = out_ref.shape[0]

    for pp in range(block):
        full = jnp.dot(weight_ref[pp], leg_ref[pp], preferred_element_type=jnp.float32)
        code = code_ref[pp]
        picked = jnp.where(code == 0, full[:channels], 0.0)
        for x in range(1, 4):
            picked = picked + jnp.where(code == x, full[x * channels : (x + 1) * channels], 0.0)
        out_ref[:, pp, :] = picked.astype(out_ref.dtype)


def legendre_inverse(legendre, spectrum, codes, block):
    pair_count, lat_count, packed = legendre.shape
    channels = spectrum.shape[0]
    return pl.pallas_call(
        inverse_kernel,
        grid=(pair_count // block,),
        in_specs=[
            pl.BlockSpec((block, lat_count, packed), lambda i: (i, 0, 0)),
            pl.BlockSpec((channels, block, packed), lambda i: (0, i, 0)),
            pl.BlockSpec((block, 1, packed), lambda i: (i, 0, 0)),
        ],
        out_specs=pl.BlockSpec((block, 2 * lat_count, 2 * channels), lambda i: (i, 0, 0)),
        out_shape=jax.ShapeDtypeStruct((pair_count, 2 * lat_count, 2 * channels), jnp.bfloat16),
    )(legendre, spectrum, codes)


def legendre_direct(legendre, weights, codes, block):
    pair_count, lat_count, packed = legendre.shape
    rows = weights.shape[1]
    channels = rows // 4
    return pl.pallas_call(
        direct_kernel,
        grid=(pair_count // block,),
        in_specs=[
            pl.BlockSpec((block, lat_count, packed), lambda i: (i, 0, 0)),
            pl.BlockSpec((block, rows, lat_count), lambda i: (i, 0, 0)),
            pl.BlockSpec((block, 1, packed), lambda i: (i, 0, 0)),
        ],
        out_specs=pl.BlockSpec((channels, block, packed), lambda i: (0, i, 0)),
        out_shape=jax.ShapeDtypeStruct((channels, pair_count, packed), jnp.bfloat16),
    )(legendre, weights, codes)


def local(spec_in, legendre, gauss_weights, row_points):
    pair_count, lat_count, packed = legendre.shape
    truncation = packed - 2
    groups = lax.axis_size("lat")
    local_channels = spec_in.shape[0]
    channels = local_channels * lax.axis_size("lev")
    block = math.gcd(pair_count, 8)
    first_pair = lax.axis_index("lat") * pair_count
    codes = slot_codes(first_pair, pair_count, packed)
    gathered = lax.all_gather(spec_in, "lev", axis=0, tiled=True)
    table, wavenumbers = wave_tables(pair_count * groups, truncation)
    gathered, table = lax.optimization_barrier((gathered, table))
    fourier = legendre_inverse(legendre, gathered, codes, block)
    fourier = fourier.reshape(pair_count, 2 * lat_count, 2, channels)
    local_rows = row_points.reshape(1, 2 * lat_count)
    band_lats = 2 * lat_count // groups
    lat_rows = lax.all_to_all(fourier, "lat", split_axis=1, concat_axis=0, tiled=True)
    my_rows = lax.dynamic_slice_in_dim(local_rows[0], lax.axis_index("lat") * band_lats, band_lats)
    answered = fourier_work(lat_rows, my_rows, table, wavenumbers, truncation)
    answered = answered.reshape(groups, pair_count, band_lats, 2, channels)
    returned = lax.all_to_all(answered, "lat", split_axis=0, concat_axis=0, tiled=True)
    back = jnp.moveaxis(returned, 0, 1).reshape(pair_count, 2 * lat_count, 2, channels)
    north_rows = back[:, :lat_count].astype(jnp.float32)
    south_rows = back[:, lat_count:].astype(jnp.float32)
    weights = gauss_weights[None, :, None, None]
    weighted = jnp.stack(
        [weights * (north_rows + south_rows), weights * (north_rows - south_rows)], axis=3
    )
    weighted = weighted.reshape(pair_count, lat_count, 4 * channels).astype(jnp.bfloat16)
    weighted = jnp.swapaxes(weighted, 1, 2)
    partial = legendre_direct(legendre, weighted, codes, block)
    return lax.psum_scatter(partial, "lev", scatter_dimension=0, tiled=True)


def solution(mesh):
    return jax.shard_map(
        local,
        mesh=mesh,
        in_specs=(P("lev", "lat", None), P("lat", "lev", None), P("lev"), P(None, "lev")),
        out_specs=P("lev", "lat", None),
        check_vma=False,
    )
```

```python
import math

import jax
import jax.numpy as jnp
from jax import lax
from jax.experimental import pallas as pl
from jax.sharding import PartitionSpec as P

NLON = 5120


def wave_tables(total_pairs, truncation):
    pair_ids = jnp.arange(total_pairs, dtype=jnp.int32)
    wavenumbers = jnp.stack([pair_ids, truncation - pair_ids], axis=1)
    flat = wavenumbers.reshape(-1)
    inner = 64
    outer = NLON // inner
    step = 2.0 * math.pi / NLON
    coarse = (flat[:, None] * (inner * jnp.arange(outer, dtype=jnp.int32))[None, :]) % NLON
    fine = (flat[:, None] * jnp.arange(inner, dtype=jnp.int32)[None, :]) % NLON
    coarse_angle = coarse.astype(jnp.float32) * step
    fine_angle = fine.astype(jnp.float32) * step
    cos_a = jnp.cos(coarse_angle)[:, :, None]
    sin_a = jnp.sin(coarse_angle)[:, :, None]
    cos_b = jnp.cos(fine_angle)[:, None, :]
    sin_b = jnp.sin(fine_angle)[:, None, :]
    rows = flat.shape[0]
    cosines = (cos_a * cos_b - sin_a * sin_b).reshape(rows, NLON).astype(jnp.bfloat16)
    sines = (sin_a * cos_b + cos_a * sin_b).reshape(rows, NLON).astype(jnp.bfloat16)
    table = lax.optimization_barrier(jnp.concatenate([cosines, sines], axis=0))
    return table, wavenumbers


def fourier_work(spectrum, row_counts, table, wavenumbers, truncation):
    pairs, lats, slots, channels = spectrum.shape
    kept_mask = (2 * wavenumbers[:, None, :] < row_counts[None, :, None]).astype(jnp.bfloat16)
    masked = spectrum * kept_mask[..., None]
    half_channels = channels // 2
    levels = half_channels // 2
    rows = lats * half_channels
    waves = pairs * slots
    flat = jnp.transpose(masked, (1, 3, 0, 2)).reshape(lats, channels, waves)
    real_part = flat[:, :half_channels].reshape(rows, waves)
    imag_part = flat[:, half_channels:].reshape(rows, waves)
    lhs = jnp.concatenate([real_part, -imag_part], axis=1)
    grid_values = jnp.dot(lhs, table, preferred_element_type=jnp.float32) * (
        1.0 / math.sqrt(truncation + 1)
    )
    grid_values = grid_values.reshape(lats, half_channels, NLON)
    vortex = grid_values[:, :levels]
    divergence = grid_values[:, levels:]
    products = jnp.concatenate(
        [vortex * divergence, 0.5 * (vortex * vortex - divergence * divergence)], axis=1
    ).astype(jnp.bfloat16)
    scale_back = 4.0 / math.sqrt(NLON)
    back = lax.dot_general(
        products.reshape(rows, NLON),
        table,
        (((1,), (1,)), ((), ())),
        preferred_element_type=jnp.float32,
    )
    real_out = back[:, :waves] * scale_back
    imag_out = back[:, waves:] * (-scale_back)
    out = jnp.concatenate(
        [real_out.reshape(lats, half_channels, waves), imag_out.reshape(lats, half_channels, waves)],
        axis=1,
    )
    out = jnp.transpose(out.reshape(lats, channels, pairs, slots), (2, 0, 3, 1))
    return (out * kept_mask[..., None].astype(jnp.float32)).astype(jnp.bfloat16)


def slot_codes(first_pair, pair_count, packed):
    pair_ids = first_pair + jnp.arange(pair_count, dtype=jnp.int32)
    positions = jnp.arange(packed, dtype=jnp.int32)
    boundary = packed - 1 - pair_ids
    in_second = (positions[None, :] >= boundary[:, None]).astype(jnp.int32)
    degree = positions[None, :] - in_second * boundary[:, None]
    return (2 * in_second + degree % 2).reshape(pair_count, 1, packed)


def inverse_kernel(leg_ref, spec_ref, factor_ref, out_ref):
    block = leg_ref.shape[0]

    for pp in range(block):
        legendre_pair = leg_ref[pp]
        spectrum = spec_ref[:, pp, :]
        factors = factor_ref[pp]
        masked = jnp.concatenate([spectrum * factors[x : x + 1] for x in range(4)], axis=0)
        sums = lax.dot_general(
            legendre_pair, masked, (((1,), (1,)), ((), ())), preferred_element_type=jnp.float32
        )
        half = sums.shape[1] // 2
        out_ref[pp] = jnp.concatenate([sums[:, :half], sums[:, half:]], axis=0).astype(
            out_ref.dtype
        )


def direct_kernel(leg_ref, weight_ref, code_ref, out_ref):
    block = leg_ref.shape[0]
    channels = out_ref.shape[0]

    for pp in range(block):
        full = jnp.dot(weight_ref[pp], leg_ref[pp], preferred_element_type=jnp.float32)
        code = code_ref[pp]
        picked = jnp.where(code == 0, full[:channels], 0.0)
        for x in range(1, 4):
            picked = picked + jnp.where(code == x, full[x * channels : (x + 1) * channels], 0.0)
        out_ref[:, pp, :] = picked.astype(out_ref.dtype)


def legendre_inverse(legendre, spectrum, codes, block):
    pair_count, lat_count, packed = legendre.shape
    channels = spectrum.shape[0]
    return pl.pallas_call(
        inverse_kernel,
        grid=(pair_count // block,),
        in_specs=[
            pl.BlockSpec((block, lat_count, packed), lambda i: (i, 0, 0)),
            pl.BlockSpec((channels, block, packed), lambda i: (0, i, 0)),
            pl.BlockSpec((block, 4, packed), lambda i: (i, 0, 0)),
        ],
        out_specs=pl.BlockSpec((block, 2 * lat_count, 2 * channels), lambda i: (i, 0, 0)),
        out_shape=jax.ShapeDtypeStruct((pair_count, 2 * lat_count, 2 * channels), jnp.bfloat16),
    )(legendre, spectrum, codes)


def legendre_direct(legendre, weights, codes, block):
    pair_count, lat_count, packed = legendre.shape
    rows = weights.shape[1]
    channels = rows // 4
    return pl.pallas_call(
        direct_kernel,
        grid=(pair_count // block,),
        in_specs=[
            pl.BlockSpec((block, lat_count, packed), lambda i: (i, 0, 0)),
            pl.BlockSpec((block, rows, lat_count), lambda i: (i, 0, 0)),
            pl.BlockSpec((block, 1, packed), lambda i: (i, 0, 0)),
        ],
        out_specs=pl.BlockSpec((channels, block, packed), lambda i: (0, i, 0)),
        out_shape=jax.ShapeDtypeStruct((channels, pair_count, packed), jnp.bfloat16),
    )(legendre, weights, codes)


def local(spec_in, legendre, gauss_weights, row_points):
    pair_count, lat_count, packed = legendre.shape
    truncation = packed - 2
    groups = lax.axis_size("lat")
    local_channels = spec_in.shape[0]
    channels = local_channels * lax.axis_size("lev")
    block = math.gcd(pair_count, 8)
    first_pair = lax.axis_index("lat") * pair_count
    codes = slot_codes(first_pair, pair_count, packed)
    gathered = lax.all_gather(spec_in, "lev", axis=0, tiled=True)
    table, wavenumbers = wave_tables(pair_count * groups, truncation)
    gathered, table = lax.optimization_barrier((gathered, table))
    slots = codes // 2
    signs = 1 - 2 * (codes % 2)
    factors = jnp.concatenate(
        [(slots == 0), (slots == 1), (slots == 0) * signs, (slots == 1) * signs], axis=1
    ).astype(jnp.bfloat16)
    fourier = legendre_inverse(legendre, gathered, factors, block)
    fourier = fourier.reshape(pair_count, 2 * lat_count, 2, channels)
    local_rows = row_points.reshape(1, 2 * lat_count)
    band_lats = 2 * lat_count // groups
    lat_rows = lax.all_to_all(fourier, "lat", split_axis=1, concat_axis=0, tiled=True)
    my_rows = lax.dynamic_slice_in_dim(local_rows[0], lax.axis_index("lat") * band_lats, band_lats)
    answered = fourier_work(lat_rows, my_rows, table, wavenumbers, truncation)
    answered = answered.reshape(groups, pair_count, band_lats, 2, channels)
    returned = lax.all_to_all(answered, "lat", split_axis=0, concat_axis=0, tiled=True)
    back = jnp.moveaxis(returned, 0, 1).reshape(pair_count, 2 * lat_count, 2, channels)
    north_rows = back[:, :lat_count].astype(jnp.float32)
    south_rows = back[:, lat_count:].astype(jnp.float32)
    weights = gauss_weights[None, :, None, None]
    weighted = jnp.stack(
        [weights * (north_rows + south_rows), weights * (north_rows - south_rows)], axis=3
    )
    weighted = weighted.reshape(pair_count, lat_count, 4 * channels).astype(jnp.bfloat16)
    weighted = jnp.swapaxes(weighted, 1, 2)
    partial = legendre_direct(legendre, weighted, codes, block)
    return lax.psum_scatter(partial, "lev", scatter_dimension=0, tiled=True)


def solution(mesh):
    return jax.shard_map(
        local,
        mesh=mesh,
        in_specs=(P("lev", "lat", None), P("lat", "lev", None), P("lev"), P(None, "lev")),
        out_specs=P("lev", "lat", None),
        check_vma=False,
    )
```

```python
import math

import jax
import jax.numpy as jnp
from jax import lax
from jax.experimental import pallas as pl
from jax.sharding import PartitionSpec as P

NLON = 5120


def wave_tables(total_pairs, truncation):
    pair_ids = jnp.arange(total_pairs, dtype=jnp.int32)
    wavenumbers = jnp.stack([pair_ids, truncation - pair_ids], axis=1)
    flat = wavenumbers.reshape(-1)
    inner = 64
    outer = NLON // inner
    step = 2.0 * math.pi / NLON
    coarse = (flat[:, None] * (inner * jnp.arange(outer, dtype=jnp.int32))[None, :]) % NLON
    fine = (flat[:, None] * jnp.arange(inner, dtype=jnp.int32)[None, :]) % NLON
    coarse_angle = coarse.astype(jnp.float32) * step
    fine_angle = fine.astype(jnp.float32) * step
    cos_a = jnp.cos(coarse_angle)[:, :, None]
    sin_a = jnp.sin(coarse_angle)[:, :, None]
    cos_b = jnp.cos(fine_angle)[:, None, :]
    sin_b = jnp.sin(fine_angle)[:, None, :]
    rows = flat.shape[0]
    cosines = (cos_a * cos_b - sin_a * sin_b).reshape(rows, NLON).astype(jnp.bfloat16)
    sines = (sin_a * cos_b + cos_a * sin_b).reshape(rows, NLON).astype(jnp.bfloat16)
    table = lax.optimization_barrier(jnp.concatenate([cosines, sines], axis=0))
    return table, wavenumbers


def fourier_work(spectrum, row_counts, table, wavenumbers, truncation):
    pairs, lats, slots, channels = spectrum.shape
    kept_mask = (2 * wavenumbers[:, None, :] < row_counts[None, :, None]).astype(jnp.bfloat16)
    masked = spectrum * kept_mask[..., None]
    half_channels = channels // 2
    levels = half_channels // 2
    rows = lats * half_channels
    waves = pairs * slots
    flat = jnp.transpose(masked, (1, 3, 0, 2)).reshape(lats, channels, waves)
    real_part = flat[:, :half_channels].reshape(rows, waves)
    imag_part = flat[:, half_channels:].reshape(rows, waves)
    lhs = jnp.concatenate([real_part, -imag_part], axis=1)
    grid_values = jnp.dot(lhs, table, preferred_element_type=jnp.float32) * (
        1.0 / math.sqrt(truncation + 1)
    )
    grid_values = grid_values.reshape(lats, half_channels, NLON)
    vortex = grid_values[:, :levels]
    divergence = grid_values[:, levels:]
    products = jnp.concatenate(
        [vortex * divergence, 0.5 * (vortex * vortex - divergence * divergence)], axis=1
    ).astype(jnp.bfloat16)
    scale_back = 4.0 / math.sqrt(NLON)
    back = lax.dot_general(
        products.reshape(rows, NLON),
        table,
        (((1,), (1,)), ((), ())),
        preferred_element_type=jnp.float32,
    )
    real_out = back[:, :waves] * scale_back
    imag_out = back[:, waves:] * (-scale_back)
    out = jnp.concatenate(
        [real_out.reshape(lats, half_channels, waves), imag_out.reshape(lats, half_channels, waves)],
        axis=1,
    )
    out = jnp.transpose(out.reshape(lats, channels, pairs, slots), (2, 0, 3, 1))
    return (out * kept_mask[..., None].astype(jnp.float32)).astype(jnp.bfloat16)


def slot_codes(first_pair, pair_count, packed):
    pair_ids = first_pair + jnp.arange(pair_count, dtype=jnp.int32)
    positions = jnp.arange(packed, dtype=jnp.int32)
    boundary = packed - 1 - pair_ids
    in_second = (positions[None, :] >= boundary[:, None]).astype(jnp.int32)
    degree = positions[None, :] - in_second * boundary[:, None]
    return (2 * in_second + degree % 2).reshape(pair_count, 1, packed)


def inverse_kernel(leg_ref, spec_ref, factor_ref, out_ref):
    block = leg_ref.shape[0]

    for pp in range(block):
        legendre_pair = leg_ref[pp]
        spectrum = spec_ref[:, pp, :]
        factors = factor_ref[pp]
        masked = jnp.concatenate([spectrum * factors[x : x + 1] for x in range(4)], axis=0)
        sums = lax.dot_general(
            legendre_pair, masked, (((1,), (1,)), ((), ())), preferred_element_type=jnp.float32
        )
        half = sums.shape[1] // 2
        out_ref[pp] = jnp.concatenate([sums[:, :half], sums[:, half:]], axis=0).astype(
            out_ref.dtype
        )


def direct_kernel(leg_ref, weight_ref, code_ref, out_ref):
    block = leg_ref.shape[0]
    channels = out_ref.shape[0]

    for pp in range(block):
        full = jnp.dot(weight_ref[pp], leg_ref[pp], preferred_element_type=jnp.float32)
        code = code_ref[pp]
        picked = jnp.where(code == 0, full[:channels], 0.0)
        for x in range(1, 4):
            picked = picked + jnp.where(code == x, full[x * channels : (x + 1) * channels], 0.0)
        out_ref[:, pp, :] = picked.astype(out_ref.dtype)


def legendre_inverse(legendre, spectrum, codes, block):
    pair_count, lat_count, packed = legendre.shape
    channels = spectrum.shape[0]
    return pl.pallas_call(
        inverse_kernel,
        grid=(pair_count // block,),
        in_specs=[
            pl.BlockSpec((block, lat_count, packed), lambda i: (i, 0, 0)),
            pl.BlockSpec((channels, block, packed), lambda i: (0, i, 0)),
            pl.BlockSpec((block, 4, packed), lambda i: (i, 0, 0)),
        ],
        out_specs=pl.BlockSpec((block, 2 * lat_count, 2 * channels), lambda i: (i, 0, 0)),
        out_shape=jax.ShapeDtypeStruct((pair_count, 2 * lat_count, 2 * channels), jnp.bfloat16),
    )(legendre, spectrum, codes)


def legendre_direct(legendre, weights, codes, block, first_block, block_count):
    pair_count, lat_count, packed = legendre.shape
    rows = weights.shape[1]
    channels = rows // 4
    return pl.pallas_call(
        direct_kernel,
        grid=(block_count,),
        in_specs=[
            pl.BlockSpec((block, lat_count, packed), lambda i: (i + first_block, 0, 0)),
            pl.BlockSpec((block, rows, lat_count), lambda i: (i + first_block, 0, 0)),
            pl.BlockSpec((block, 1, packed), lambda i: (i + first_block, 0, 0)),
        ],
        out_specs=pl.BlockSpec((channels, block, packed), lambda i: (0, i, 0)),
        out_shape=jax.ShapeDtypeStruct((channels, block * block_count, packed), jnp.bfloat16),
    )(legendre, weights, codes)


def local(spec_in, legendre, gauss_weights, row_points):
    pair_count, lat_count, packed = legendre.shape
    truncation = packed - 2
    groups = lax.axis_size("lat")
    local_channels = spec_in.shape[0]
    channels = local_channels * lax.axis_size("lev")
    block = math.gcd(pair_count, 8)
    first_pair = lax.axis_index("lat") * pair_count
    codes = slot_codes(first_pair, pair_count, packed)
    gathered = lax.all_gather(spec_in, "lev", axis=0, tiled=True)
    table, wavenumbers = wave_tables(pair_count * groups, truncation)
    gathered, table = lax.optimization_barrier((gathered, table))
    slots = codes // 2
    signs = 1 - 2 * (codes % 2)
    factors = jnp.concatenate(
        [(slots == 0), (slots == 1), (slots == 0) * signs, (slots == 1) * signs], axis=1
    ).astype(jnp.bfloat16)
    fourier = legendre_inverse(legendre, gathered, factors, block)
    fourier = fourier.reshape(pair_count, 2 * lat_count, 2, channels)
    local_rows = row_points.reshape(1, 2 * lat_count)
    band_lats = 2 * lat_count // groups
    lat_rows = lax.all_to_all(fourier, "lat", split_axis=1, concat_axis=0, tiled=True)
    my_rows = lax.dynamic_slice_in_dim(local_rows[0], lax.axis_index("lat") * band_lats, band_lats)
    answered = fourier_work(lat_rows, my_rows, table, wavenumbers, truncation)
    answered = answered.reshape(groups, pair_count, band_lats, 2, channels)
    returned = lax.all_to_all(answered, "lat", split_axis=0, concat_axis=0, tiled=True)
    back = jnp.moveaxis(returned, 0, 1).reshape(pair_count, 2 * lat_count, 2, channels)
    north_rows = back[:, :lat_count].astype(jnp.float32)
    south_rows = back[:, lat_count:].astype(jnp.float32)
    weights = gauss_weights[None, :, None, None]
    weighted = jnp.stack(
        [weights * (north_rows + south_rows), weights * (north_rows - south_rows)], axis=3
    )
    weighted = weighted.reshape(pair_count, lat_count, 4 * channels).astype(jnp.bfloat16)
    weighted = jnp.swapaxes(weighted, 1, 2)
    blocks = pair_count // block
    first_half = blocks // 2
    halves = []
    for first_block, block_count in ((0, first_half), (first_half, blocks - first_half)):
        partial = legendre_direct(legendre, weighted, codes, block, first_block, block_count)
        halves.append(lax.psum_scatter(partial, "lev", scatter_dimension=0, tiled=True))
    return jnp.concatenate(halves, axis=1)


def solution(mesh):
    return jax.shard_map(
        local,
        mesh=mesh,
        in_specs=(P("lev", "lat", None), P("lat", "lev", None), P("lev"), P(None, "lev")),
        out_specs=P("lev", "lat", None),
        check_vma=False,
    )
```

```python
import math

import jax
import jax.numpy as jnp
from jax import lax
from jax.experimental import pallas as pl
from jax.sharding import PartitionSpec as P

NLON = 5120


def wave_tables(total_pairs, truncation):
    pair_ids = jnp.arange(total_pairs, dtype=jnp.int32)
    wavenumbers = jnp.stack([pair_ids, truncation - pair_ids], axis=1)
    flat = wavenumbers.reshape(-1)
    inner = 64
    outer = NLON // inner
    step = 2.0 * math.pi / NLON
    coarse = (flat[:, None] * (inner * jnp.arange(outer, dtype=jnp.int32))[None, :]) % NLON
    fine = (flat[:, None] * jnp.arange(inner, dtype=jnp.int32)[None, :]) % NLON
    coarse_angle = coarse.astype(jnp.float32) * step
    fine_angle = fine.astype(jnp.float32) * step
    cos_a = jnp.cos(coarse_angle)[:, :, None]
    sin_a = jnp.sin(coarse_angle)[:, :, None]
    cos_b = jnp.cos(fine_angle)[:, None, :]
    sin_b = jnp.sin(fine_angle)[:, None, :]
    rows = flat.shape[0]
    cosines = (cos_a * cos_b - sin_a * sin_b).reshape(rows, NLON).astype(jnp.bfloat16)
    sines = (sin_a * cos_b + cos_a * sin_b).reshape(rows, NLON).astype(jnp.bfloat16)
    table = lax.optimization_barrier(jnp.concatenate([cosines, sines], axis=0))
    return table, wavenumbers


def fourier_work(spectrum, row_counts, table, wavenumbers, truncation):
    pairs, lats, slots, channels = spectrum.shape
    kept_mask = (2 * wavenumbers[:, None, :] < row_counts[None, :, None]).astype(jnp.bfloat16)
    masked = spectrum
    half_channels = channels // 2
    levels = half_channels // 2
    rows = lats * half_channels
    waves = pairs * slots
    flat = jnp.transpose(masked, (1, 3, 0, 2)).reshape(lats, channels, waves)
    real_part = flat[:, :half_channels].reshape(rows, waves)
    imag_part = flat[:, half_channels:].reshape(rows, waves)
    lhs = jnp.concatenate([real_part, -imag_part], axis=1)
    grid_values = jnp.dot(lhs, table, preferred_element_type=jnp.float32) * (
        1.0 / math.sqrt(truncation + 1)
    )
    grid_values = grid_values.reshape(lats, half_channels, NLON)
    vortex = grid_values[:, :levels]
    divergence = grid_values[:, levels:]
    products = jnp.concatenate(
        [vortex * divergence, 0.5 * (vortex * vortex - divergence * divergence)], axis=1
    ).astype(jnp.bfloat16)
    scale_back = 4.0 / math.sqrt(NLON)
    back = lax.dot_general(
        products.reshape(rows, NLON),
        table,
        (((1,), (1,)), ((), ())),
        preferred_element_type=jnp.float32,
    )
    real_out = back[:, :waves] * scale_back
    imag_out = back[:, waves:] * (-scale_back)
    out = jnp.concatenate(
        [real_out.reshape(lats, half_channels, waves), imag_out.reshape(lats, half_channels, waves)],
        axis=1,
    )
    out = jnp.transpose(out.reshape(lats, channels, pairs, slots), (2, 0, 3, 1))
    return (out * kept_mask[..., None].astype(jnp.float32)).astype(jnp.bfloat16)


def slot_codes(first_pair, pair_count, packed):
    pair_ids = first_pair + jnp.arange(pair_count, dtype=jnp.int32)
    positions = jnp.arange(packed, dtype=jnp.int32)
    boundary = packed - 1 - pair_ids
    in_second = (positions[None, :] >= boundary[:, None]).astype(jnp.int32)
    degree = positions[None, :] - in_second * boundary[:, None]
    return (2 * in_second + degree % 2).reshape(pair_count, 1, packed)


def inverse_kernel(leg_ref, spec_ref, factor_ref, out_ref):
    block = leg_ref.shape[0]

    for pp in range(block):
        legendre_pair = leg_ref[pp]
        spectrum = spec_ref[:, pp, :]
        factors = factor_ref[pp]
        masked = jnp.concatenate([spectrum * factors[x : x + 1] for x in range(4)], axis=0)
        sums = lax.dot_general(
            legendre_pair, masked, (((1,), (1,)), ((), ())), preferred_element_type=jnp.float32
        )
        half = sums.shape[1] // 2
        out_ref[pp] = jnp.concatenate([sums[:, :half], sums[:, half:]], axis=0).astype(
            out_ref.dtype
        )


def direct_kernel(leg_ref, weight_ref, code_ref, out_ref):
    block = leg_ref.shape[0]
    channels = out_ref.shape[0]

    for pp in range(block):
        full = jnp.dot(weight_ref[pp], leg_ref[pp], preferred_element_type=jnp.float32)
        code = code_ref[pp]
        picked = jnp.where(code == 0, full[:channels], 0.0)
        for x in range(1, 4):
            picked = picked + jnp.where(code == x, full[x * channels : (x + 1) * channels], 0.0)
        out_ref[:, pp, :] = picked.astype(out_ref.dtype)


def legendre_inverse(legendre, spectrum, codes, block):
    pair_count, lat_count, packed = legendre.shape
    channels = spectrum.shape[0]
    return pl.pallas_call(
        inverse_kernel,
        grid=(pair_count // block,),
        in_specs=[
            pl.BlockSpec((block, lat_count, packed), lambda i: (i, 0, 0)),
            pl.BlockSpec((channels, block, packed), lambda i: (0, i, 0)),
            pl.BlockSpec((block, 4, packed), lambda i: (i, 0, 0)),
        ],
        out_specs=pl.BlockSpec((block, 2 * lat_count, 2 * channels), lambda i: (i, 0, 0)),
        out_shape=jax.ShapeDtypeStruct((pair_count, 2 * lat_count, 2 * channels), jnp.bfloat16),
    )(legendre, spectrum, codes)


def legendre_direct(legendre, weights, codes, block):
    pair_count, lat_count, packed = legendre.shape
    rows = weights.shape[1]
    channels = rows // 4
    return pl.pallas_call(
        direct_kernel,
        grid=(pair_count // block,),
        in_specs=[
            pl.BlockSpec((block, lat_count, packed), lambda i: (i, 0, 0)),
            pl.BlockSpec((block, rows, lat_count), lambda i: (i, 0, 0)),
            pl.BlockSpec((block, 1, packed), lambda i: (i, 0, 0)),
        ],
        out_specs=pl.BlockSpec((channels, block, packed), lambda i: (0, i, 0)),
        out_shape=jax.ShapeDtypeStruct((channels, pair_count, packed), jnp.bfloat16),
    )(legendre, weights, codes)


def local(spec_in, legendre, gauss_weights, row_points):
    pair_count, lat_count, packed = legendre.shape
    truncation = packed - 2
    groups = lax.axis_size("lat")
    local_channels = spec_in.shape[0]
    channels = local_channels * lax.axis_size("lev")
    block = math.gcd(pair_count, 8)
    first_pair = lax.axis_index("lat") * pair_count
    codes = slot_codes(first_pair, pair_count, packed)
    gathered = lax.all_gather(spec_in, "lev", axis=0, tiled=True)
    table, wavenumbers = wave_tables(pair_count * groups, truncation)
    gathered, table = lax.optimization_barrier((gathered, table))
    slots = codes // 2
    signs = 1 - 2 * (codes % 2)
    factors = jnp.concatenate(
        [(slots == 0), (slots == 1), (slots == 0) * signs, (slots == 1) * signs], axis=1
    ).astype(jnp.bfloat16)
    fourier = legendre_inverse(legendre, gathered, factors, block)
    fourier = fourier.reshape(pair_count, 2 * lat_count, 2, channels)
    own_waves = lax.dynamic_slice_in_dim(wavenumbers, first_pair, pair_count)
    own_rows = row_points.reshape(2 * lat_count)
    own_kept = (2 * own_waves[:, None, :] < own_rows[None, :, None]).astype(jnp.bfloat16)
    fourier = fourier * own_kept[..., None]
    local_rows = row_points.reshape(1, 2 * lat_count)
    band_lats = 2 * lat_count // groups
    lat_rows = lax.all_to_all(fourier, "lat", split_axis=1, concat_axis=0, tiled=True)
    my_rows = lax.dynamic_slice_in_dim(local_rows[0], lax.axis_index("lat") * band_lats, band_lats)
    answered = fourier_work(lat_rows, my_rows, table, wavenumbers, truncation)
    answered = answered.reshape(groups, pair_count, band_lats, 2, channels)
    returned = lax.all_to_all(answered, "lat", split_axis=0, concat_axis=0, tiled=True)
    back = jnp.moveaxis(returned, 0, 1).reshape(pair_count, 2 * lat_count, 2, channels)
    north_rows = back[:, :lat_count].astype(jnp.float32)
    south_rows = back[:, lat_count:].astype(jnp.float32)
    weights = gauss_weights[None, :, None, None]
    weighted = jnp.stack(
        [weights * (north_rows + south_rows), weights * (north_rows - south_rows)], axis=3
    )
    weighted = weighted.reshape(pair_count, lat_count, 4 * channels).astype(jnp.bfloat16)
    weighted = jnp.swapaxes(weighted, 1, 2)
    partial = legendre_direct(legendre, weighted, codes, block)
    return lax.psum_scatter(partial, "lev", scatter_dimension=0, tiled=True)


def solution(mesh):
    return jax.shard_map(
        local,
        mesh=mesh,
        in_specs=(P("lev", "lat", None), P("lat", "lev", None), P("lev"), P(None, "lev")),
        out_specs=P("lev", "lat", None),
        check_vma=False,
    )
```

```python
import math

import jax
import jax.numpy as jnp
from jax import lax
from jax.experimental import pallas as pl
from jax.sharding import PartitionSpec as P

NLON = 5120


def wave_tables(total_pairs, truncation):
    pair_ids = jnp.arange(total_pairs, dtype=jnp.int32)
    wavenumbers = jnp.stack([pair_ids, truncation - pair_ids], axis=1)
    flat = wavenumbers.reshape(-1)
    inner = 64
    outer = NLON // inner
    step = 2.0 * math.pi / NLON
    coarse = (flat[:, None] * (inner * jnp.arange(outer, dtype=jnp.int32))[None, :]) % NLON
    fine = (flat[:, None] * jnp.arange(inner, dtype=jnp.int32)[None, :]) % NLON
    coarse_angle = coarse.astype(jnp.float32) * step
    fine_angle = fine.astype(jnp.float32) * step
    cos_a = jnp.cos(coarse_angle)[:, :, None]
    sin_a = jnp.sin(coarse_angle)[:, :, None]
    cos_b = jnp.cos(fine_angle)[:, None, :]
    sin_b = jnp.sin(fine_angle)[:, None, :]
    rows = flat.shape[0]
    cosines = (cos_a * cos_b - sin_a * sin_b).reshape(rows, NLON).astype(jnp.bfloat16)
    sines = (sin_a * cos_b + cos_a * sin_b).reshape(rows, NLON).astype(jnp.bfloat16)
    table = lax.optimization_barrier(jnp.concatenate([cosines, sines], axis=0))
    return table, wavenumbers


def fourier_work(spectrum, row_counts, table, wavenumbers, truncation):
    pairs, lats, slots, channels = spectrum.shape
    kept_mask = (2 * wavenumbers[:, None, :] < row_counts[None, :, None]).astype(jnp.bfloat16)
    masked = spectrum * kept_mask[..., None]
    half_channels = channels // 2
    levels = half_channels // 2
    rows = lats * half_channels
    waves = pairs * slots
    flat = jnp.transpose(masked, (1, 3, 0, 2)).reshape(lats, channels, waves)
    real_part = flat[:, :half_channels].reshape(rows, waves)
    imag_part = flat[:, half_channels:].reshape(rows, waves)
    lhs = jnp.concatenate([real_part, -imag_part], axis=1)
    grid_values = jnp.dot(lhs, table, preferred_element_type=jnp.float32) * (
        1.0 / math.sqrt(truncation + 1)
    )
    grid_values = grid_values.reshape(lats, half_channels, NLON)
    vortex = grid_values[:, :levels]
    divergence = grid_values[:, levels:]
    products = jnp.concatenate(
        [vortex * divergence, 0.5 * (vortex * vortex - divergence * divergence)], axis=1
    ).astype(jnp.bfloat16)
    scale_back = 4.0 / math.sqrt(NLON)
    back = lax.dot_general(
        products.reshape(rows, NLON),
        table,
        (((1,), (1,)), ((), ())),
        preferred_element_type=jnp.float32,
    )
    real_out = back[:, :waves] * scale_back
    imag_out = back[:, waves:] * (-scale_back)
    out = jnp.concatenate(
        [real_out.reshape(lats, half_channels, waves), imag_out.reshape(lats, half_channels, waves)],
        axis=1,
    )
    out = jnp.transpose(out.reshape(lats, channels, pairs, slots), (2, 0, 3, 1))
    return (out * kept_mask[..., None].astype(jnp.float32)).astype(jnp.bfloat16)


def slot_codes(first_pair, pair_count, packed):
    pair_ids = first_pair + jnp.arange(pair_count, dtype=jnp.int32)
    positions = jnp.arange(packed, dtype=jnp.int32)
    boundary = packed - 1 - pair_ids
    in_second = (positions[None, :] >= boundary[:, None]).astype(jnp.int32)
    degree = positions[None, :] - in_second * boundary[:, None]
    return (2 * in_second + degree % 2).reshape(pair_count, 1, packed)


def inverse_kernel(leg_ref, spec_ref, factor_ref, out_ref):
    block = leg_ref.shape[0]

    for pp in range(block):
        legendre_pair = leg_ref[pp]
        spectrum = spec_ref[:, pp, :]
        factors = factor_ref[pp]
        masked = jnp.concatenate([spectrum * factors[x : x + 1] for x in range(4)], axis=0)
        sums = lax.dot_general(
            legendre_pair, masked, (((1,), (1,)), ((), ())), preferred_element_type=jnp.float32
        )
        half = sums.shape[1] // 2
        out_ref[pp] = jnp.concatenate([sums[:, :half], sums[:, half:]], axis=0).astype(
            out_ref.dtype
        )


def direct_kernel(leg_ref, weight_ref, code_ref, out_ref):
    block = leg_ref.shape[0]
    channels = out_ref.shape[0]

    for pp in range(block):
        full = jnp.dot(weight_ref[pp], leg_ref[pp], preferred_element_type=jnp.float32)
        code = code_ref[pp]
        picked = jnp.where(code == 0, full[:channels], 0.0)
        for x in range(1, 4):
            picked = picked + jnp.where(code == x, full[x * channels : (x + 1) * channels], 0.0)
        out_ref[:, pp, :] = picked.astype(out_ref.dtype)


def legendre_inverse(legendre, spectrum, codes, block):
    pair_count, lat_count, packed = legendre.shape
    channels = spectrum.shape[0]
    return pl.pallas_call(
        inverse_kernel,
        grid=(pair_count // block,),
        in_specs=[
            pl.BlockSpec((block, lat_count, packed), lambda i: (i, 0, 0)),
            pl.BlockSpec((channels, block, packed), lambda i: (0, i, 0)),
            pl.BlockSpec((block, 4, packed), lambda i: (i, 0, 0)),
        ],
        out_specs=pl.BlockSpec((block, 2 * lat_count, 2 * channels), lambda i: (i, 0, 0)),
        out_shape=jax.ShapeDtypeStruct((pair_count, 2 * lat_count, 2 * channels), jnp.bfloat16),
    )(legendre, spectrum, codes)


def legendre_direct(legendre, weights, codes, block):
    pair_count, lat_count, packed = legendre.shape
    rows = weights.shape[1]
    channels = rows // 4
    return pl.pallas_call(
        direct_kernel,
        grid=(pair_count // block,),
        in_specs=[
            pl.BlockSpec((block, lat_count, packed), lambda i: (i, 0, 0)),
            pl.BlockSpec((block, rows, lat_count), lambda i: (i, 0, 0)),
            pl.BlockSpec((block, 1, packed), lambda i: (i, 0, 0)),
        ],
        out_specs=pl.BlockSpec((channels, block, packed), lambda i: (0, i, 0)),
        out_shape=jax.ShapeDtypeStruct((channels, pair_count, packed), jnp.bfloat16),
    )(legendre, weights, codes)


def local(spec_in, legendre, gauss_weights, row_points):
    pair_count, lat_count, packed = legendre.shape
    truncation = packed - 2
    groups = lax.axis_size("lat")
    local_channels = spec_in.shape[0]
    channels = local_channels * lax.axis_size("lev")
    block = math.gcd(pair_count, 8)
    first_pair = lax.axis_index("lat") * pair_count
    codes = slot_codes(first_pair, pair_count, packed)
    gathered = lax.all_gather(spec_in, "lev", axis=0, tiled=True)
    table, wavenumbers = wave_tables(pair_count * groups, truncation)
    gathered, table = lax.optimization_barrier((gathered, table))
    slots = codes // 2
    signs = 1 - 2 * (codes % 2)
    factors = jnp.concatenate(
        [(slots == 0), (slots == 1), (slots == 0) * signs, (slots == 1) * signs], axis=1
    ).astype(jnp.bfloat16)
    fourier = legendre_inverse(legendre, gathered, factors, block)
    fourier = fourier.reshape(pair_count, 2 * lat_count, 2, channels)
    local_rows = row_points.reshape(1, 2 * lat_count)
    band_lats = 2 * lat_count // groups
    lat_rows = lax.all_to_all(fourier, "lat", split_axis=1, concat_axis=0, tiled=True)
    my_rows = lax.dynamic_slice_in_dim(local_rows[0], lax.axis_index("lat") * band_lats, band_lats)
    answered = fourier_work(lat_rows, my_rows, table, wavenumbers, truncation)
    answered = answered.reshape(groups, pair_count, band_lats, 2, channels)
    returned = lax.all_to_all(answered, "lat", split_axis=0, concat_axis=0, tiled=True)
    back = jnp.moveaxis(returned, 0, 1).reshape(pair_count, 2 * lat_count, 2, channels)
    north_rows = back[:, :lat_count].astype(jnp.float32)
    south_rows = back[:, lat_count:].astype(jnp.float32)
    weights = gauss_weights[None, :, None, None]
    weighted = jnp.stack(
        [weights * (north_rows + south_rows), weights * (north_rows - south_rows)], axis=3
    )
    weighted = weighted.reshape(pair_count, lat_count, 4 * channels).astype(jnp.bfloat16)
    weighted = jnp.swapaxes(weighted, 1, 2)
    partial = legendre_direct(legendre, weighted, codes, block)
    summed = lax.psum(partial, "lev")
    return lax.dynamic_slice_in_dim(summed, lax.axis_index("lev") * local_channels, local_channels, 0)


def solution(mesh):
    return jax.shard_map(
        local,
        mesh=mesh,
        in_specs=(P("lev", "lat", None), P("lat", "lev", None), P("lev"), P(None, "lev")),
        out_specs=P("lev", "lat", None),
        check_vma=False,
    )
```

```python
import math

import jax
import jax.numpy as jnp
from jax import lax
from jax.experimental import pallas as pl
from jax.sharding import PartitionSpec as P

NLON = 5120


def wave_tables(total_pairs, truncation):
    pair_ids = jnp.arange(total_pairs, dtype=jnp.int32)
    wavenumbers = jnp.stack([pair_ids, truncation - pair_ids], axis=1)
    flat = wavenumbers.reshape(-1)
    inner = 64
    outer = NLON // inner
    step = 2.0 * math.pi / NLON
    coarse = (flat[:, None] * (inner * jnp.arange(outer, dtype=jnp.int32))[None, :]) % NLON
    fine = (flat[:, None] * jnp.arange(inner, dtype=jnp.int32)[None, :]) % NLON
    coarse_angle = coarse.astype(jnp.float32) * step
    fine_angle = fine.astype(jnp.float32) * step
    cos_a = jnp.cos(coarse_angle)[:, :, None]
    sin_a = jnp.sin(coarse_angle)[:, :, None]
    cos_b = jnp.cos(fine_angle)[:, None, :]
    sin_b = jnp.sin(fine_angle)[:, None, :]
    rows = flat.shape[0]
    cosines = (cos_a * cos_b - sin_a * sin_b).reshape(rows, NLON).astype(jnp.bfloat16)
    sines = (sin_a * cos_b + cos_a * sin_b).reshape(rows, NLON).astype(jnp.bfloat16)
    table = lax.optimization_barrier(jnp.concatenate([cosines, sines], axis=0))
    return table, wavenumbers


def fourier_work(spectrum, row_counts, table, wavenumbers, truncation):
    pairs, lats, slots, channels = spectrum.shape
    kept_mask = (2 * wavenumbers[:, None, :] < row_counts[None, :, None]).astype(jnp.bfloat16)
    masked = spectrum * kept_mask[..., None]
    half_channels = channels // 2
    levels = half_channels // 2
    rows = lats * half_channels
    waves = pairs * slots
    flat = jnp.transpose(masked, (1, 3, 0, 2)).reshape(lats, channels, waves)
    real_part = flat[:, :half_channels].reshape(rows, waves)
    imag_part = flat[:, half_channels:].reshape(rows, waves)
    lhs = jnp.concatenate([real_part, -imag_part], axis=1)
    grid_values = jnp.dot(lhs, table, preferred_element_type=jnp.float32) * (
        1.0 / math.sqrt(truncation + 1)
    )
    grid_values = grid_values.reshape(lats, half_channels, NLON)
    vortex = grid_values[:, :levels]
    divergence = grid_values[:, levels:]
    products = jnp.concatenate(
        [vortex * divergence, 0.5 * (vortex * vortex - divergence * divergence)], axis=1
    ).astype(jnp.bfloat16)
    scale_back = 4.0 / math.sqrt(NLON)
    back = lax.dot_general(
        products.reshape(rows, NLON),
        table,
        (((1,), (1,)), ((), ())),
        preferred_element_type=jnp.float32,
    )
    real_out = back[:, :waves] * scale_back
    imag_out = back[:, waves:] * (-scale_back)
    out = jnp.concatenate(
        [real_out.reshape(lats, half_channels, waves), imag_out.reshape(lats, half_channels, waves)],
        axis=1,
    )
    out = jnp.transpose(out.reshape(lats, channels, pairs, slots), (2, 0, 3, 1))
    return (out * kept_mask[..., None].astype(jnp.float32)).astype(jnp.bfloat16)


def slot_codes(first_pair, pair_count, packed):
    pair_ids = first_pair + jnp.arange(pair_count, dtype=jnp.int32)
    positions = jnp.arange(packed, dtype=jnp.int32)
    boundary = packed - 1 - pair_ids
    in_second = (positions[None, :] >= boundary[:, None]).astype(jnp.int32)
    degree = positions[None, :] - in_second * boundary[:, None]
    return (2 * in_second + degree % 2).reshape(pair_count, 1, packed)


def inverse_kernel(leg_ref, spec_ref, factor_ref, out_ref):
    block = leg_ref.shape[0]

    for pp in range(block):
        legendre_pair = leg_ref[pp]
        spectrum = spec_ref[:, pp, :]
        factors = factor_ref[pp]
        masked = jnp.concatenate([spectrum * factors[x : x + 1] for x in range(4)], axis=0)
        sums = lax.dot_general(
            legendre_pair, masked, (((1,), (1,)), ((), ())), preferred_element_type=jnp.float32
        )
        half = sums.shape[1] // 2
        out_ref[pp] = jnp.concatenate([sums[:, :half], sums[:, half:]], axis=0).astype(
            out_ref.dtype
        )


def direct_kernel(leg_ref, weight_ref, code_ref, out_ref):
    block = leg_ref.shape[0]
    channels = out_ref.shape[0]

    for pp in range(block):
        full = jnp.dot(weight_ref[pp], leg_ref[pp], preferred_element_type=jnp.float32)
        factors = code_ref[pp]
        picked = full[:channels] * factors[0:1]
        for x in range(1, 4):
            picked = picked + full[x * channels : (x + 1) * channels] * factors[x : x + 1]
        out_ref[:, pp, :] = picked.astype(out_ref.dtype)


def legendre_inverse(legendre, spectrum, codes, block):
    pair_count, lat_count, packed = legendre.shape
    channels = spectrum.shape[0]
    return pl.pallas_call(
        inverse_kernel,
        grid=(pair_count // block,),
        in_specs=[
            pl.BlockSpec((block, lat_count, packed), lambda i: (i, 0, 0)),
            pl.BlockSpec((channels, block, packed), lambda i: (0, i, 0)),
            pl.BlockSpec((block, 4, packed), lambda i: (i, 0, 0)),
        ],
        out_specs=pl.BlockSpec((block, 2 * lat_count, 2 * channels), lambda i: (i, 0, 0)),
        out_shape=jax.ShapeDtypeStruct((pair_count, 2 * lat_count, 2 * channels), jnp.bfloat16),
    )(legendre, spectrum, codes)


def legendre_direct(legendre, weights, codes, block):
    pair_count, lat_count, packed = legendre.shape
    rows = weights.shape[1]
    channels = rows // 4
    return pl.pallas_call(
        direct_kernel,
        grid=(pair_count // block,),
        in_specs=[
            pl.BlockSpec((block, lat_count, packed), lambda i: (i, 0, 0)),
            pl.BlockSpec((block, rows, lat_count), lambda i: (i, 0, 0)),
            pl.BlockSpec((block, 4, packed), lambda i: (i, 0, 0)),
        ],
        out_specs=pl.BlockSpec((channels, block, packed), lambda i: (0, i, 0)),
        out_shape=jax.ShapeDtypeStruct((channels, pair_count, packed), jnp.bfloat16),
    )(legendre, weights, codes)


def local(spec_in, legendre, gauss_weights, row_points):
    pair_count, lat_count, packed = legendre.shape
    truncation = packed - 2
    groups = lax.axis_size("lat")
    local_channels = spec_in.shape[0]
    channels = local_channels * lax.axis_size("lev")
    block = math.gcd(pair_count, 8)
    first_pair = lax.axis_index("lat") * pair_count
    codes = slot_codes(first_pair, pair_count, packed)
    gathered = lax.all_gather(spec_in, "lev", axis=0, tiled=True)
    table, wavenumbers = wave_tables(pair_count * groups, truncation)
    gathered, table = lax.optimization_barrier((gathered, table))
    slots = codes // 2
    signs = 1 - 2 * (codes % 2)
    factors = jnp.concatenate(
        [(slots == 0), (slots == 1), (slots == 0) * signs, (slots == 1) * signs], axis=1
    ).astype(jnp.bfloat16)
    fourier = legendre_inverse(legendre, gathered, factors, block)
    fourier = fourier.reshape(pair_count, 2 * lat_count, 2, channels)
    local_rows = row_points.reshape(1, 2 * lat_count)
    band_lats = 2 * lat_count // groups
    lat_rows = lax.all_to_all(fourier, "lat", split_axis=1, concat_axis=0, tiled=True)
    my_rows = lax.dynamic_slice_in_dim(local_rows[0], lax.axis_index("lat") * band_lats, band_lats)
    answered = fourier_work(lat_rows, my_rows, table, wavenumbers, truncation)
    answered = answered.reshape(groups, pair_count, band_lats, 2, channels)
    returned = lax.all_to_all(answered, "lat", split_axis=0, concat_axis=0, tiled=True)
    back = jnp.moveaxis(returned, 0, 1).reshape(pair_count, 2 * lat_count, 2, channels)
    north_rows = back[:, :lat_count].astype(jnp.float32)
    south_rows = back[:, lat_count:].astype(jnp.float32)
    weights = gauss_weights[None, :, None, None]
    weighted = jnp.stack(
        [weights * (north_rows + south_rows), weights * (north_rows - south_rows)], axis=3
    )
    weighted = weighted.reshape(pair_count, lat_count, 4 * channels).astype(jnp.bfloat16)
    weighted = jnp.swapaxes(weighted, 1, 2)
    picks = (codes == jnp.arange(4, dtype=jnp.int32)[None, :, None]).astype(jnp.float32)
    partial = legendre_direct(legendre, weighted, picks, block)
    return lax.psum_scatter(partial, "lev", scatter_dimension=0, tiled=True)


def solution(mesh):
    return jax.shard_map(
        local,
        mesh=mesh,
        in_specs=(P("lev", "lat", None), P("lat", "lev", None), P("lev"), P(None, "lev")),
        out_specs=P("lev", "lat", None),
        check_vma=False,
    )
```
